128 devices in a mesh: tm: 32 (over x, y, core), chan: 4 (over z).
Axes of the slice: x: 4, y: 4, z: 4, core: 2. Of those that a mesh axis runs over, the one named last changes fastest.
Arguments:
- streams: bfloat16 [262144, 1024], P('tm', 'chan'), may hold values from -6 to 6
- weights: bfloat16 [262144, 1024], P('tm', 'chan'), may hold values from 0.25 to 4
- pointing: int32 [262144], P('tm'), may hold values from 0 to 127
- touched: int32 [32, 32], replicated, may hold values from 0 to 3
- foreground_modes: float32 [1024, 16], P('chan'), as said below
Outputs:
- map_cube: float32 [16384, 1024], P('tm', 'chan')
- residual: float32 [16384, 1024], P('tm', 'chan')
The draws below stay inside these ranges and needn't reach their ends.
Inputs may be any that keep to these rules, and one draw needn't show every extreme that they name: `foreground_modes`: the columns are mutually orthogonal over the 1024 channels, each of norm at most one.
All inputs are finite; a program needn't handle non-finite values.
Results may differ from the reference program's by a relative error of at most 0.0006.
Values may be sent and summed in bfloat16 or wider, within the bound.
No kernel may reach another device: no remote copies, remote signals or barrier semaphores. Data moves between devices by JAX's collectives and lax.ppermute only.
A program may use at most 128 MiB of HBM per device.

```python
import math
import jax
import jax.numpy as jnp
import numpy as np
from jax import lax

CH = 1024
MODES = 16
PIX_DEV = 512
BLK = 128
S_DEV = 8192
ITERS = 3
NPIX = 16384
BPD = 4
TOTAL = 262144
N_TM = 32


def draw_foreground_modes(key, part):
    frequency = (jax.random.permutation(key, CH - 1)[:MODES] + 1).astype(jnp.int32)
    channel = jnp.arange(CH, dtype=jnp.int32)
    phase = (2 * channel[:, None] + 1) * frequency[None, :] % (4 * CH)
    columns = math.sqrt(2.0 / CH) * jnp.cos(math.pi * phase.astype(jnp.float32) / (2.0 * CH))
    return columns.astype(jnp.float32)


def set_ends(result, stream_key, smallest, high):
    place = [jax.random.randint(jax.random.fold_in(stream_key, axis), (), 0, length) for axis, length in enumerate(result.shape)]
    widest = result.shape.index(max(result.shape))
    beside = place[:widest] + [(place[widest] + 1) % result.shape[widest]] + place[widest + 1:]
    return result.at[tuple(place)].set(smallest).at[tuple(beside)].set(high)


def levels(own_key, shape, pieces, low, high):
    def one(axis_at, blocks):
        heights = jax.random.uniform(jax.random.fold_in(jax.random.fold_in(own_key, 6), axis_at), (blocks,), jnp.float32, low / len(pieces), high / len(pieces))
        return jnp.repeat(jnp.exp(heights), shape[axis_at] // blocks).reshape((-1,) + (1,) * (len(shape) - axis_at - 1))

    factor_of = one(*pieces[0])
    for cut in pieces[1:]:
        factor_of = factor_of * one(*cut)
    return factor_of


def cumulative_ranks(count, lean):
    weights = [(1 << 20) // math.isqrt(standing ** lean) + 1 for standing in range(1, count + 1)]
    scale = 1 + sum(weights) // (1 << 30)
    return np.cumsum(np.array([max(1, weight // scale) for weight in weights]))


def ranked(own_key, shape, count, slope):
    table = cumulative_ranks(count, slope)
    ticket = jax.random.randint(jax.random.fold_in(own_key, 1), shape, 0, int(table[count - 1]))
    standing = jnp.searchsorted(jnp.asarray(table, jnp.int32), ticket, side="right")
    return jax.random.permutation(jax.random.fold_in(own_key, 2), count)[standing].astype(jnp.int32)


def scatter_about(key, shape, spread, bound, pieces=(), kind=jnp.bfloat16):
    drawn = spread * jax.random.normal(key, shape, jnp.float32)
    if pieces:
        drawn = drawn * levels(key, shape, pieces, -0.22, 0.18)
    return jnp.clip(drawn, -bound, bound).astype(kind)


def setup_inputs(seed: int = 0) -> dict:
    streams_of = jax.random.split(jax.random.key(seed), 6)
    streams = scatter_about(streams_of[0], (TOTAL, CH), 1.0, 6.0, ((0, 32), (1, 4)))
    weights = jnp.clip(jnp.exp(math.log(4.0) - 2.7725887 * jax.random.uniform(streams_of[1], (TOTAL, CH), jnp.float32) ** levels(streams_of[1], (TOTAL, CH), ((0, 32), (1, 4)), -0.2, 0.2)), 0.25, 4.0).astype(jnp.bfloat16)
    pointing = set_ends(ranked(streams_of[2], (TOTAL,), BLK, 1), jax.random.fold_in(streams_of[2], 3), 0, BLK - 1).astype(jnp.int32)
    touched = set_ends(jax.random.randint(streams_of[3], (N_TM, N_TM), 0, BPD), jax.random.fold_in(streams_of[3], 1), 0, BPD - 1).astype(jnp.int32)
    foreground_modes = draw_foreground_modes(jax.random.fold_in(streams_of[5], 71), 0)
    return dict(streams=streams, weights=weights, pointing=pointing, touched=touched, foreground_modes=foreground_modes)


ridge = 1.0


def reference(streams, weights, pointing, touched, foreground_modes):
    run_length = S_DEV // N_TM
    owner_run = (jnp.arange(S_DEV, dtype=jnp.int32) // run_length).astype(jnp.int32)
    group_streams = streams.reshape(N_TM, S_DEV, CH)
    group_weights = weights.reshape(N_TM, S_DEV, CH)
    group_points = pointing.reshape(N_TM, S_DEV).astype(jnp.int32)
    seen = jnp.take_along_axis(touched.astype(jnp.int32), jnp.broadcast_to(owner_run[None, :], (N_TM, S_DEV)), axis=1)
    pixels = (owner_run[None, :] * PIX_DEV + seen * BLK + group_points).astype(jnp.int32)

    def noise(samples, scale_in):
        scale = scale_in.astype(jnp.float32)
        weighted = scale * samples
        amplitudes = jnp.dot(weighted, foreground_modes, precision=lax.Precision.HIGHEST)
        return scale * (weighted - jnp.dot(amplitudes, foreground_modes.T, precision=lax.Precision.HIGHEST))

    def operate(field):
        def visit(summed, item):
            where, scale = item
            return summed.at[where].add(noise(field[where], scale)), None
        summed, unused = lax.scan(visit, jnp.zeros((NPIX, CH), jnp.float32), (pixels, group_weights))
        return summed + ridge * field

    def visit_streams(summed, item):
        where, scale, group = item
        return summed.at[where].add(noise(group.astype(jnp.float32), scale)), None

    right_side, unused = lax.scan(visit_streams, jnp.zeros((NPIX, CH), jnp.float32), (pixels, group_weights, group_streams))
    map_cube = jnp.zeros_like(right_side)
    residual = right_side
    direction = right_side
    norm_now = jnp.sum(residual * residual)
    for iteration in range(ITERS):
        applied = operate(direction)
        step_size = norm_now / jnp.sum(direction * applied)
        map_cube = map_cube + step_size * direction
        residual = residual - step_size * applied
        norm_next = jnp.sum(residual * residual)
        direction = residual + (norm_next / norm_now) * direction
        norm_now = norm_next
    return map_cube, residual
```

```python
import jax
import jax.numpy as jnp
from jax import lax
from jax.sharding import PartitionSpec as P

PIX_DEV = 512
BLK = 128
ITERS = 3


highest = lax.Precision.HIGHEST
ridge = 1.0


def chan_sum(value):
    count = lax.axis_size("chan")
    total = value
    for shift in range(1, count):
        pairs = [(i, (i + shift) % count) for i in range(count)]
        total = total + lax.ppermute(value, "chan", pairs)
    return total


def global_sum(value):
    chans = lax.axis_size("chan")
    got = lax.all_to_all(jnp.broadcast_to(value, (chans, 1)), "chan", 0, 0, tiled=True)
    part = jnp.sum(got)
    groups = lax.axis_size("tm")
    got = lax.all_to_all(jnp.broadcast_to(part, (groups, 1)), "tm", 0, 0, tiled=True)
    return jnp.sum(got)


def per_device(streams, weights, pointing, touched, foreground_modes):
    group_count = lax.axis_size("tm")
    owner_index = lax.axis_index("tm")
    sample_count, channels = streams.shape
    run_length = sample_count // group_count
    blocks_each = PIX_DEV // BLK

    runs = streams.reshape(group_count, run_length, channels)
    scales = weights.reshape(group_count, run_length, channels)
    points = pointing.reshape(group_count, run_length)
    if run_length == channels:
        packed = jnp.concatenate(
            [runs, scales, points.astype(jnp.bfloat16)[:, None, :]], axis=1
        )
        packed = lax.all_to_all(packed, "tm", 0, 0, tiled=True)
        runs_in = packed[:, :run_length]
        weights_in = packed[:, run_length : 2 * run_length]
        points_in = packed[:, 2 * run_length].astype(jnp.int32)
    else:
        runs_in = lax.all_to_all(runs, "tm", 0, 0, tiled=True)
        weights_in = lax.all_to_all(scales, "tm", 0, 0, tiled=True)
        points_in = lax.all_to_all(points, "tm", 0, 0, tiled=True)

    column = lax.dynamic_index_in_dim(touched, owner_index, axis=1, keepdims=False)
    owned_blocks = (column[:, None] == jnp.arange(blocks_each, dtype=jnp.int32)[None, :]).astype(
        jnp.float32
    )
    pixel_hits = (points_in[:, :, None] == jnp.arange(BLK, dtype=jnp.int32)[None, None, :]).astype(
        jnp.float32
    )
    noise_weights = weights_in.astype(jnp.float32)

    def filtered(samples):
        weighted = noise_weights * samples
        amplitudes = jnp.einsum("csk,km->mcs", weighted, foreground_modes, precision=highest)
        amplitudes = chan_sum(amplitudes)
        return noise_weights * (
            weighted - jnp.einsum("mcs,km->csk", amplitudes, foreground_modes, precision=highest)
        )

    def binned(samples):
        partial_value = jnp.einsum("csp,csk->cpk", pixel_hits, samples, precision=highest)
        summed = jnp.einsum("cb,cpk->bpk", owned_blocks, partial_value, precision=highest)
        return summed.reshape(PIX_DEV, channels)

    def pointed(field):
        picked = jnp.einsum(
            "cb,bpk->cpk",
            owned_blocks,
            field.reshape(blocks_each, BLK, channels),
            precision=highest,
        )
        return jnp.einsum("csp,cpk->csk", pixel_hits, picked, precision=highest)

    def squares(vector):
        return global_sum(jnp.sum(vector * vector))

    right_side = binned(filtered(runs_in.astype(jnp.float32)))
    map_cube = jnp.zeros_like(right_side)
    residual = right_side
    direction = right_side
    norm_now = squares(residual)
    for iteration in range(ITERS):
        applied = binned(filtered(pointed(direction))) + ridge * direction
        step_size = norm_now / global_sum(jnp.sum(direction * applied))
        map_cube = map_cube + step_size * direction
        residual = residual - step_size * applied
        norm_next = squares(residual)
        direction = residual + norm_next / norm_now * direction
        norm_now = norm_next
    return (map_cube, residual)


def solution(mesh):
    in_specs = (P("tm", "chan"), P("tm", "chan"), P("tm"), P(), P("chan", None))
    out_specs = (P("tm", "chan"), P("tm", "chan"))
    return jax.shard_map(
        per_device, mesh=mesh, in_specs=in_specs, out_specs=out_specs, check_vma=False
    )
```

```python
import jax
import jax.numpy as jnp
from jax import lax
from jax.sharding import PartitionSpec as P

PIX_DEV = 512
BLK = 128
ITERS = 3


highest = lax.Precision.HIGHEST
high = lax.Precision.HIGH
ridge = 1.0


def chan_sum(value):
    count = lax.axis_size("chan")
    total = value
    for shift in range(1, count):
        pairs = [(i, (i + shift) % count) for i in range(count)]
        total = total + lax.ppermute(value, "chan", pairs)
    return total


def global_sum(value):
    everyone = lax.axis_size("tm") * lax.axis_size("chan")
    got = lax.all_to_all(
        jnp.broadcast_to(value, (everyone, 1)), ("tm", "chan"), 0, 0, tiled=True
    )
    return jnp.sum(got)


def per_device(streams, weights, pointing, touched, foreground_modes):
    group_count = lax.axis_size("tm")
    owner_index = lax.axis_index("tm")
    sample_count, channels = streams.shape
    run_length = sample_count // group_count
    blocks_each = PIX_DEV // BLK

    runs = streams.reshape(group_count, run_length, channels)
    scales = weights.reshape(group_count, run_length, channels)
    points = pointing.reshape(group_count, run_length)
    if run_length == channels:
        packed = jnp.concatenate(
            [runs, scales, points.astype(jnp.bfloat16)[:, None, :]], axis=1
        )
        packed = lax.all_to_all(packed, "tm", 0, 0, tiled=True)
        runs_in = packed[:, :run_length]
        weights_in = packed[:, run_length : 2 * run_length]
        points_in = packed[:, 2 * run_length].astype(jnp.int32)
    else:
        runs_in = lax.all_to_all(runs, "tm", 0, 0, tiled=True)
        weights_in = lax.all_to_all(scales, "tm", 0, 0, tiled=True)
        points_in = lax.all_to_all(points, "tm", 0, 0, tiled=True)

    column = lax.dynamic_index_in_dim(touched, owner_index, axis=1, keepdims=False)
    owned_blocks = (column[:, None] == jnp.arange(blocks_each, dtype=jnp.int32)[None, :]).astype(
        jnp.float32
    )
    pixel_hits = (points_in[:, :, None] == jnp.arange(BLK, dtype=jnp.int32)[None, None, :]).astype(
        jnp.float32
    )
    noise_weights = weights_in.astype(jnp.float32)

    def filtered(samples):
        weighted = noise_weights * samples
        amplitudes = jnp.einsum("csk,km->mcs", weighted, foreground_modes, precision=highest)
        amplitudes = chan_sum(amplitudes)
        return noise_weights * (
            weighted - jnp.einsum("mcs,km->csk", amplitudes, foreground_modes, precision=highest)
        )

    def binned(samples):
        partial_value = jnp.einsum("csp,csk->cpk", pixel_hits, samples, precision=high)
        summed = jnp.einsum("cb,cpk->bpk", owned_blocks, partial_value, precision=high)
        return summed.reshape(PIX_DEV, channels)

    def pointed(field):
        picked = jnp.einsum(
            "cb,bpk->cpk",
            owned_blocks,
            field.reshape(blocks_each, BLK, channels),
            precision=high,
        )
        return jnp.einsum("csp,cpk->csk", pixel_hits, picked, precision=high)

    def squares(vector):
        return global_sum(jnp.sum(vector * vector))

    right_side = binned(filtered(runs_in.astype(jnp.float32)))
    map_cube = jnp.zeros_like(right_side)
    residual = right_side
    direction = right_side
    norm_now = squares(residual)
    for iteration in range(ITERS):
        applied = binned(filtered(pointed(direction))) + ridge * direction
        step_size = norm_now / global_sum(jnp.sum(direction * applied))
        map_cube = map_cube + step_size * direction
        residual = residual - step_size * applied
        norm_next = squares(residual)
        direction = residual + norm_next / norm_now * direction
        norm_now = norm_next
    return (map_cube, residual)


def solution(mesh):
    in_specs = (P("tm", "chan"), P("tm", "chan"), P("tm"), P(), P("chan", None))
    out_specs = (P("tm", "chan"), P("tm", "chan"))
    return jax.shard_map(
        per_device, mesh=mesh, in_specs=in_specs, out_specs=out_specs, check_vma=False
    )
```

```python
import jax
import jax.numpy as jnp
from jax import lax
from jax.sharding import PartitionSpec as P

PIX_DEV = 512
BLK = 128
ITERS = 3


highest = lax.Precision.HIGHEST
high = lax.Precision.HIGH
ridge = 1.0


def chan_sum(value):
    count = lax.axis_size("chan")
    total = value
    for shift in range(1, count):
        pairs = [(i, (i + shift) % count) for i in range(count)]
        total = total + lax.ppermute(value, "chan", pairs)
    return total


def global_sum(value):
    everyone = lax.axis_size("tm") * lax.axis_size("chan")
    got = lax.all_to_all(
        jnp.broadcast_to(value, (everyone, 1)), ("tm", "chan"), 0, 0, tiled=True
    )
    return jnp.sum(got)


def per_device(streams, weights, pointing, touched, foreground_modes):
    group_count = lax.axis_size("tm")
    owner_index = lax.axis_index("tm")
    sample_count, channels = streams.shape
    run_length = sample_count // group_count
    blocks_each = PIX_DEV // BLK

    runs = streams.reshape(group_count, run_length, channels)
    scales = weights.reshape(group_count, run_length, channels)
    points = pointing.reshape(group_count, run_length)
    if run_length == channels:
        packed = jnp.concatenate(
            [runs, scales, points.astype(jnp.bfloat16)[:, None, :]], axis=1
        )
        packed = lax.all_to_all(packed, "tm", 0, 0, tiled=True)
        runs_in = packed[:, :run_length]
        weights_in = packed[:, run_length : 2 * run_length]
        points_in = packed[:, 2 * run_length].astype(jnp.int32)
    else:
        runs_in = lax.all_to_all(runs, "tm", 0, 0, tiled=True)
        weights_in = lax.all_to_all(scales, "tm", 0, 0, tiled=True)
        points_in = lax.all_to_all(points, "tm", 0, 0, tiled=True)

    column = lax.dynamic_index_in_dim(touched, owner_index, axis=1, keepdims=False)
    owned_blocks = (column[:, None] == jnp.arange(blocks_each, dtype=jnp.int32)[None, :]).astype(
        jnp.float32
    )
    pixel_hits = (points_in[:, :, None] == jnp.arange(BLK, dtype=jnp.int32)[None, None, :]).astype(
        jnp.float32
    )
    noise_weights = weights_in.astype(jnp.float32)

    def filtered(samples):
        weighted = noise_weights * samples
        amplitudes = jnp.einsum("csk,km->mcs", weighted, foreground_modes, precision=highest)
        amplitudes = chan_sum(amplitudes)
        return noise_weights * (
            weighted - jnp.einsum("mcs,km->csk", amplitudes, foreground_modes, precision=highest)
        )

    def binned(samples):
        partial_value = jnp.einsum("csp,csk->cpk", pixel_hits, samples, precision=high)
        summed = jnp.einsum("cb,cpk->bpk", owned_blocks, partial_value, precision=high)
        return summed.reshape(PIX_DEV, channels)

    def pointed(field):
        picked = jnp.einsum(
            "cb,bpk->cpk",
            owned_blocks,
            field.reshape(blocks_each, BLK, channels),
            precision=high,
        )
        return jnp.einsum("csp,cpk->csk", pixel_hits, picked, precision=high)

    def squares(vector):
        return global_sum(jnp.sum(vector * vector))

    def operate(field):
        return binned(filtered(pointed(field))) + ridge * field

    right_side = binned(filtered(runs_in.astype(jnp.float32)))
    map_cube = jnp.zeros_like(right_side)
    residual = right_side
    direction = right_side
    norm_now = squares(residual)
    applied = operate(direction)
    for iteration in range(ITERS):
        step_size = norm_now / global_sum(jnp.sum(direction * applied))
        map_cube = map_cube + step_size * direction
        residual = residual - step_size * applied
        if iteration == ITERS - 1:
            break
        norm_next = squares(residual)
        applied_residual = operate(residual)
        ratio = norm_next / norm_now
        direction = residual + ratio * direction
        applied = applied_residual + ratio * applied
        norm_now = norm_next
    return (map_cube, residual)


def solution(mesh):
    in_specs = (P("tm", "chan"), P("tm", "chan"), P("tm"), P(), P("chan", None))
    out_specs = (P("tm", "chan"), P("tm", "chan"))
    return jax.shard_map(
        per_device, mesh=mesh, in_specs=in_specs, out_specs=out_specs, check_vma=False
    )
```

```python
import jax
import jax.numpy as jnp
from jax import lax
from jax.sharding import PartitionSpec as P

PIX_DEV = 512
BLK = 128
ITERS = 3


highest = lax.Precision.HIGHEST
high = lax.Precision.HIGH
ridge = 1.0


def chan_sum(value):
    count = lax.axis_size("chan")
    total = value
    for shift in range(1, count):
        pairs = [(i, (i + shift) % count) for i in range(count)]
        total = total + lax.ppermute(value, "chan", pairs)
    return total


def global_sum(value):
    everyone = lax.axis_size("tm") * lax.axis_size("chan")
    got = lax.all_to_all(
        jnp.broadcast_to(value, (everyone, 1)), ("tm", "chan"), 0, 0, tiled=True
    )
    return jnp.sum(got)


def per_device(streams, weights, pointing, touched, foreground_modes):
    group_count = lax.axis_size("tm")
    owner_index = lax.axis_index("tm")
    sample_count, channels = streams.shape
    run_length = sample_count // group_count
    blocks_each = PIX_DEV // BLK

    scales = weights.reshape(group_count, run_length, channels)
    points = pointing.reshape(group_count, run_length)
    if run_length == channels:
        packed = jnp.concatenate([scales, points.astype(jnp.bfloat16)[:, None, :]], axis=1)
        packed = lax.all_to_all(packed, "tm", 0, 0, tiled=True)
        weights_in = packed[:, :run_length]
        points_in = packed[:, run_length].astype(jnp.int32)
    else:
        weights_in = lax.all_to_all(scales, "tm", 0, 0, tiled=True)
        points_in = lax.all_to_all(points, "tm", 0, 0, tiled=True)

    column = lax.dynamic_index_in_dim(touched, owner_index, axis=1, keepdims=False)
    owned_blocks = (column[:, None] == jnp.arange(blocks_each, dtype=jnp.int32)[None, :]).astype(
        jnp.float32
    )
    pixel_hits = (points_in[:, :, None] == jnp.arange(BLK, dtype=jnp.int32)[None, None, :]).astype(
        jnp.float32
    )
    noise_weights = weights_in.astype(jnp.float32)

    def filtered(samples, noise_weights):
        weighted = noise_weights * samples
        amplitudes = jnp.einsum("csk,km->mcs", weighted, foreground_modes, precision=highest)
        amplitudes = chan_sum(amplitudes)
        return noise_weights * (
            weighted - jnp.einsum("mcs,km->csk", amplitudes, foreground_modes, precision=highest)
        )

    def binned(samples):
        partial_value = jnp.einsum("csp,csk->cpk", pixel_hits, samples, precision=high)
        summed = jnp.einsum("cb,cpk->bpk", owned_blocks, partial_value, precision=high)
        return summed.reshape(PIX_DEV, channels)

    def pointed(field):
        picked = jnp.einsum(
            "cb,bpk->cpk",
            owned_blocks,
            field.reshape(blocks_each, BLK, channels),
            precision=high,
        )
        return jnp.einsum("csp,cpk->csk", pixel_hits, picked, precision=high)

    def squares(vector):
        return global_sum(jnp.sum(vector * vector))

    def operate(field):
        return binned(filtered(pointed(field), noise_weights)) + ridge * field

    local_hits = (points[:, :, None] == jnp.arange(BLK, dtype=jnp.int32)[None, None, :]).astype(
        jnp.float32
    )
    local_noise = filtered(
        streams.astype(jnp.float32).reshape(group_count, run_length, channels),
        scales.astype(jnp.float32),
    )
    local_partial = jnp.einsum("csp,csk->cpk", local_hits, local_noise, precision=high)
    arrived = lax.all_to_all(local_partial, "tm", 0, 0, tiled=True)
    right_side = jnp.einsum("cb,cpk->bpk", owned_blocks, arrived, precision=high).reshape(
        PIX_DEV, channels
    )
    map_cube = jnp.zeros_like(right_side)
    residual = right_side
    direction = right_side
    norm_now = squares(residual)
    applied = operate(direction)
    for iteration in range(ITERS):
        step_size = norm_now / global_sum(jnp.sum(direction * applied))
        map_cube = map_cube + step_size * direction
        residual = residual - step_size * applied
        if iteration == ITERS - 1:
            break
        norm_next = squares(residual)
        applied_residual = operate(residual)
        ratio = norm_next / norm_now
        direction = residual + ratio * direction
        applied = applied_residual + ratio * applied
        norm_now = norm_next
    return (map_cube, residual)


def solution(mesh):
    in_specs = (P("tm", "chan"), P("tm", "chan"), P("tm"), P(), P("chan", None))
    out_specs = (P("tm", "chan"), P("tm", "chan"))
    return jax.shard_map(
        per_device, mesh=mesh, in_specs=in_specs, out_specs=out_specs, check_vma=False
    )
```

```python
import functools

import jax
import jax.numpy as jnp
from jax import lax
from jax.experimental import pallas as pl
from jax.experimental.pallas import tpu as pltpu
from jax.sharding import PartitionSpec as P

PIX_DEV = 512
BLK = 128
ITERS = 3


highest = lax.Precision.HIGHEST
high = lax.Precision.HIGH
ridge = 1.0
RUNS = 4


def gathered(field_ref, block, points):
    start = pl.multiple_of(block * BLK, BLK)
    rest = field_ref[pl.ds(start, BLK), :]
    hits = (points == lax.broadcasted_iota(jnp.int32, (points.shape[0], BLK), 1)).astype(
        jnp.bfloat16
    )
    total = None
    for _ in range(3):
        part = rest.astype(jnp.bfloat16)
        rest = rest - part.astype(jnp.float32)
        term = jnp.dot(hits, part, preferred_element_type=jnp.float32)
        total = term if total is None else total + term
    return total


def amp_kernel(blocks_ref, field_ref, points_ref, weights_ref, modes_t_ref, amp_ref):
    step = pl.program_id(0)
    for j in range(RUNS):
        x = gathered(field_ref, blocks_ref[step * RUNS + j], points_ref[j])
        y = weights_ref[j].astype(jnp.float32) * x
        amp_ref[j] = lax.dot_general(
            modes_t_ref[...], y, (((1,), (1,)), ((), ())),
            precision=highest, preferred_element_type=jnp.float32,
        )


def bin_kernel(blocks_ref, field_ref, points_ref, rows_ref, weights_ref, amp_ref, modes_t_ref, out_ref):
    step = pl.program_id(0)

    @pl.when(step == 0)
    def _():
        out_ref[...] = jnp.zeros_like(out_ref)

    for j in range(RUNS):
        block = blocks_ref[step * RUNS + j]
        x = gathered(field_ref, block, points_ref[j])
        w = weights_ref[j].astype(jnp.float32)
        y = w * x
        correction = lax.dot_general(
            amp_ref[j], modes_t_ref[...], (((0,), (0,)), ((), ())),
            precision=highest, preferred_element_type=jnp.float32,
        )
        rest = w * (y - correction)
        hits = (rows_ref[j] == lax.broadcasted_iota(jnp.int32, (BLK, rest.shape[0]), 0)).astype(
            jnp.bfloat16
        )
        total = None
        for _ in range(3):
            part = rest.astype(jnp.bfloat16)
            rest = rest - part.astype(jnp.float32)
            term = jnp.dot(hits, part, preferred_element_type=jnp.float32)
            total = term if total is None else total + term
        start = pl.multiple_of(block * BLK, BLK)
        out_ref[pl.ds(start, BLK), :] += total


def owner_operator(blocks, field, points_col, points_row, noise_weights, modes_t):
    groups, run_length, channels = noise_weights.shape
    modes = modes_t.shape[0]
    steps = groups // RUNS
    full = pl.BlockSpec(field.shape, lambda i, b: (0, 0))
    per_run = lambda *shape: pl.BlockSpec((RUNS,) + shape, lambda i, b: (i, 0, 0))
    gather_flops = groups * 3 * 2 * run_length * BLK * channels
    amps = pl.pallas_call(
        amp_kernel,
        grid_spec=pltpu.PrefetchScalarGridSpec(
            num_scalar_prefetch=1,
            grid=(steps,),
            in_specs=[full, per_run(run_length, 1), per_run(run_length, channels),
                      pl.BlockSpec(modes_t.shape, lambda i, b: (0, 0))],
            out_specs=per_run(modes, run_length),
        ),
        out_shape=jax.ShapeDtypeStruct((groups, modes, run_length), jnp.float32),
        cost_estimate=pl.CostEstimate(
            flops=gather_flops + groups * 12 * run_length * channels * modes,
            bytes_accessed=noise_weights.size * 2 + field.size * 4,
            transcendentals=0,
        ),
    )(blocks, field, points_col, noise_weights, modes_t)
    amps = chan_sum(amps)
    return pl.pallas_call(
        bin_kernel,
        grid_spec=pltpu.PrefetchScalarGridSpec(
            num_scalar_prefetch=1,
            grid=(steps,),
            in_specs=[full, per_run(run_length, 1), per_run(1, run_length),
                      per_run(run_length, channels), per_run(modes, run_length),
                      pl.BlockSpec(modes_t.shape, lambda i, b: (0, 0))],
            out_specs=full,
        ),
        out_shape=jax.ShapeDtypeStruct(field.shape, jnp.float32),
        cost_estimate=pl.CostEstimate(
            flops=2 * gather_flops + groups * 12 * run_length * channels * modes,
            bytes_accessed=noise_weights.size * 2 + field.size * 8,
            transcendentals=0,
        ),
    )(blocks, field, points_col, points_row, noise_weights, amps, modes_t)


def chan_sum(value):
    count = lax.axis_size("chan")
    total = value
    for shift in range(1, count):
        pairs = [(i, (i + shift) % count) for i in range(count)]
        total = total + lax.ppermute(value, "chan", pairs)
    return total


def global_sum(value):
    everyone = lax.axis_size("tm") * lax.axis_size("chan")
    got = lax.all_to_all(
        jnp.broadcast_to(value, (everyone, 1)), ("tm", "chan"), 0, 0, tiled=True
    )
    return jnp.sum(got)


def per_device(streams, weights, pointing, touched, foreground_modes):
    group_count = lax.axis_size("tm")
    owner_index = lax.axis_index("tm")
    sample_count, channels = streams.shape
    run_length = sample_count // group_count
    blocks_each = PIX_DEV // BLK

    scales = weights.reshape(group_count, run_length, channels)
    points = pointing.reshape(group_count, run_length)
    if run_length == channels:
        packed = jnp.concatenate([scales, points.astype(jnp.bfloat16)[:, None, :]], axis=1)
        packed = lax.all_to_all(packed, "tm", 0, 0, tiled=True)
        weights_in = packed[:, :run_length]
        points_in = packed[:, run_length].astype(jnp.int32)
    else:
        weights_in = lax.all_to_all(scales, "tm", 0, 0, tiled=True)
        points_in = lax.all_to_all(points, "tm", 0, 0, tiled=True)

    column = lax.dynamic_index_in_dim(touched, owner_index, axis=1, keepdims=False)
    owned_blocks = (column[:, None] == jnp.arange(blocks_each, dtype=jnp.int32)[None, :]).astype(
        jnp.float32
    )
    pixel_hits = (points_in[:, :, None] == jnp.arange(BLK, dtype=jnp.int32)[None, None, :]).astype(
        jnp.float32
    )
    noise_weights = weights_in.astype(jnp.float32)

    def filtered(samples, noise_weights):
        weighted = noise_weights * samples
        amplitudes = jnp.einsum("csk,km->mcs", weighted, foreground_modes, precision=highest)
        amplitudes = chan_sum(amplitudes)
        return noise_weights * (
            weighted - jnp.einsum("mcs,km->csk", amplitudes, foreground_modes, precision=highest)
        )

    def binned(samples):
        partial_value = jnp.einsum("csp,csk->cpk", pixel_hits, samples, precision=high)
        summed = jnp.einsum("cb,cpk->bpk", owned_blocks, partial_value, precision=high)
        return summed.reshape(PIX_DEV, channels)

    def pointed(field):
        picked = jnp.einsum(
            "cb,bpk->cpk",
            owned_blocks,
            field.reshape(blocks_each, BLK, channels),
            precision=high,
        )
        return jnp.einsum("csp,cpk->csk", pixel_hits, picked, precision=high)

    def squares(vector):
        return global_sum(jnp.sum(vector * vector))

    points_col = points_in[:, :, None]
    points_row = points_in[:, None, :]
    modes_t = foreground_modes.T

    def operate(field):
        return (
            owner_operator(column, field, points_col, points_row, weights_in, modes_t)
            + ridge * field
        )

    local_hits = (points[:, :, None] == jnp.arange(BLK, dtype=jnp.int32)[None, None, :]).astype(
        jnp.float32
    )
    local_noise = filtered(
        streams.astype(jnp.float32).reshape(group_count, run_length, channels),
        scales.astype(jnp.float32),
    )
    local_partial = jnp.einsum("csp,csk->cpk", local_hits, local_noise, precision=high)
    arrived = lax.all_to_all(local_partial, "tm", 0, 0, tiled=True)
    right_side = jnp.einsum("cb,cpk->bpk", owned_blocks, arrived, precision=high).reshape(
        PIX_DEV, channels
    )
    map_cube = jnp.zeros_like(right_side)
    residual = right_side
    direction = right_side
    norm_now = squares(residual)
    applied = operate(direction)
    for iteration in range(ITERS):
        step_size = norm_now / global_sum(jnp.sum(direction * applied))
        map_cube = map_cube + step_size * direction
        residual = residual - step_size * applied
        if iteration == ITERS - 1:
            break
        norm_next = squares(residual)
        applied_residual = operate(residual)
        ratio = norm_next / norm_now
        direction = residual + ratio * direction
        applied = applied_residual + ratio * applied
        norm_now = norm_next
    return (map_cube, residual)


def solution(mesh):
    in_specs = (P("tm", "chan"), P("tm", "chan"), P("tm"), P(), P("chan", None))
    out_specs = (P("tm", "chan"), P("tm", "chan"))
    return jax.shard_map(
        per_device, mesh=mesh, in_specs=in_specs, out_specs=out_specs, check_vma=False
    )
```

```python
import functools

import jax
import jax.numpy as jnp
from jax import lax
from jax.experimental import pallas as pl
from jax.experimental.pallas import tpu as pltpu
from jax.sharding import PartitionSpec as P

PIX_DEV = 512
BLK = 128
ITERS = 3


highest = lax.Precision.HIGHEST
high = lax.Precision.HIGH
ridge = 1.0
RUNS = 4


def gathered(parts_ref, block, hits):
    start = pl.multiple_of(block * BLK, BLK)
    total = None
    for k in range(3):
        term = jnp.dot(hits, parts_ref[k, pl.ds(start, BLK), :], preferred_element_type=jnp.float32)
        total = term if total is None else total + term
    return total


def amp_kernel(blocks_ref, parts_ref, hits_ref, weights_ref, modes_t_ref, amp_ref):
    step = pl.program_id(0)
    for j in range(RUNS):
        x = gathered(parts_ref, blocks_ref[step * RUNS + j], hits_ref[j])
        y = weights_ref[j].astype(jnp.float32) * x
        amp_ref[j] = lax.dot_general(
            modes_t_ref[...], y, (((1,), (1,)), ((), ())),
            precision=highest, preferred_element_type=jnp.float32,
        )


def bin_kernel(blocks_ref, parts_ref, hits_ref, rows_ref, weights_ref, amp_ref, modes_t_ref, out_ref):
    step = pl.program_id(0)

    @pl.when(step == 0)
    def _():
        out_ref[...] = jnp.zeros_like(out_ref)

    for j in range(RUNS):
        block = blocks_ref[step * RUNS + j]
        x = gathered(parts_ref, block, hits_ref[j])
        w = weights_ref[j].astype(jnp.float32)
        correction = lax.dot_general(
            amp_ref[j], modes_t_ref[...], (((0,), (0,)), ((), ())),
            precision=highest, preferred_element_type=jnp.float32,
        )
        rest = w * (w * x - correction)
        hits = (rows_ref[j] == lax.broadcasted_iota(jnp.int32, (BLK, rest.shape[0]), 0)).astype(
            jnp.bfloat16
        )
        high_part = rest.astype(jnp.bfloat16)
        low_part = (rest - high_part.astype(jnp.float32)).astype(jnp.bfloat16)
        total = jnp.dot(hits, high_part, preferred_element_type=jnp.float32) + jnp.dot(
            hits, low_part, preferred_element_type=jnp.float32
        )
        start = pl.multiple_of(block * BLK, BLK)
        out_ref[pl.ds(start, BLK), :] += total


def owner_operator(blocks, field, hits, points_row, noise_weights, modes_t):
    groups, run_length, channels = noise_weights.shape
    modes = modes_t.shape[0]
    steps = groups // RUNS
    parts = []
    rest = field
    for _ in range(3):
        rounded = lax.reduce_precision(rest, exponent_bits=8, mantissa_bits=7)
        parts.append(rounded.astype(jnp.bfloat16))
        rest = rest - rounded
    parts = jnp.stack(parts)
    full = pl.BlockSpec(parts.shape, lambda i, b: (0, 0, 0))
    per_run = lambda *shape: pl.BlockSpec((RUNS,) + shape, lambda i, b: (i, 0, 0))
    gather_flops = groups * 3 * 2 * run_length * BLK * channels
    amps = pl.pallas_call(
        amp_kernel,
        grid_spec=pltpu.PrefetchScalarGridSpec(
            num_scalar_prefetch=1,
            grid=(steps,),
            in_specs=[full, per_run(run_length, BLK), per_run(run_length, channels),
                      pl.BlockSpec(modes_t.shape, lambda i, b: (0, 0))],
            out_specs=per_run(modes, run_length),
        ),
        out_shape=jax.ShapeDtypeStruct((groups, modes, run_length), jnp.float32),
        cost_estimate=pl.CostEstimate(
            flops=gather_flops + groups * 12 * run_length * channels * modes,
            bytes_accessed=noise_weights.size * 2 + field.size * 4,
            transcendentals=0,
        ),
    )(blocks, parts, hits, noise_weights, modes_t)
    amps = chan_sum(amps)
    return pl.pallas_call(
        bin_kernel,
        grid_spec=pltpu.PrefetchScalarGridSpec(
            num_scalar_prefetch=1,
            grid=(steps,),
            in_specs=[full, per_run(run_length, BLK), per_run(1, run_length),
                      per_run(run_length, channels), per_run(modes, run_length),
                      pl.BlockSpec(modes_t.shape, lambda i, b: (0, 0))],
            out_specs=pl.BlockSpec(field.shape, lambda i, b: (0, 0)),
        ),
        out_shape=jax.ShapeDtypeStruct(field.shape, jnp.float32),
        cost_estimate=pl.CostEstimate(
            flops=2 * gather_flops + groups * 12 * run_length * channels * modes,
            bytes_accessed=noise_weights.size * 2 + field.size * 8,
            transcendentals=0,
        ),
    )(blocks, parts, hits, points_row, noise_weights, amps, modes_t)


def chan_sum(value):
    count = lax.axis_size("chan")
    total = value
    for shift in range(1, count):
        pairs = [(i, (i + shift) % count) for i in range(count)]
        total = total + lax.ppermute(value, "chan", pairs)
    return total


def global_sum(value):
    everyone = lax.axis_size("tm") * lax.axis_size("chan")
    got = lax.all_to_all(
        jnp.broadcast_to(value, (everyone, 1)), ("tm", "chan"), 0, 0, tiled=True
    )
    return jnp.sum(got)


def per_device(streams, weights, pointing, touched, foreground_modes):
    group_count = lax.axis_size("tm")
    owner_index = lax.axis_index("tm")
    sample_count, channels = streams.shape
    run_length = sample_count // group_count
    blocks_each = PIX_DEV // BLK

    scales = weights.reshape(group_count, run_length, channels)
    points = pointing.reshape(group_count, run_length)
    if run_length == channels:
        packed = jnp.concatenate([scales, points.astype(jnp.bfloat16)[:, None, :]], axis=1)
        packed = lax.all_to_all(packed, "tm", 0, 0, tiled=True)
        weights_in = packed[:, :run_length]
        points_in = packed[:, run_length].astype(jnp.int32)
    else:
        weights_in = lax.all_to_all(scales, "tm", 0, 0, tiled=True)
        points_in = lax.all_to_all(points, "tm", 0, 0, tiled=True)

    column = lax.dynamic_index_in_dim(touched, owner_index, axis=1, keepdims=False)
    owned_blocks = (column[:, None] == jnp.arange(blocks_each, dtype=jnp.int32)[None, :]).astype(
        jnp.float32
    )
    pixel_hits = (points_in[:, :, None] == jnp.arange(BLK, dtype=jnp.int32)[None, None, :]).astype(
        jnp.float32
    )
    noise_weights = weights_in.astype(jnp.float32)

    def filtered(samples, noise_weights):
        weighted = noise_weights * samples
        amplitudes = jnp.einsum("csk,km->mcs", weighted, foreground_modes, precision=highest)
        amplitudes = chan_sum(amplitudes)
        return noise_weights * (
            weighted - jnp.einsum("mcs,km->csk", amplitudes, foreground_modes, precision=highest)
        )

    def binned(samples):
        partial_value = jnp.einsum("csp,csk->cpk", pixel_hits, samples, precision=high)
        summed = jnp.einsum("cb,cpk->bpk", owned_blocks, partial_value, precision=high)
        return summed.reshape(PIX_DEV, channels)

    def pointed(field):
        picked = jnp.einsum(
            "cb,bpk->cpk",
            owned_blocks,
            field.reshape(blocks_each, BLK, channels),
            precision=high,
        )
        return jnp.einsum("csp,cpk->csk", pixel_hits, picked, precision=high)

    def squares(vector):
        return global_sum(jnp.sum(vector * vector))

    point_hits = (points_in[:, :, None] == jnp.arange(BLK, dtype=jnp.int32)[None, None, :]).astype(
        jnp.bfloat16
    )
    points_row = points_in[:, None, :]
    modes_t = foreground_modes.T

    def operate(field):
        return (
            owner_operator(column, field, point_hits, points_row, weights_in, modes_t)
            + ridge * field
        )

    local_hits = (points[:, :, None] == jnp.arange(BLK, dtype=jnp.int32)[None, None, :]).astype(
        jnp.float32
    )
    local_noise = filtered(
        streams.astype(jnp.float32).reshape(group_count, run_length, channels),
        scales.astype(jnp.float32),
    )
    local_partial = jnp.einsum("csp,csk->cpk", local_hits, local_noise, precision=high)
    arrived = lax.all_to_all(local_partial, "tm", 0, 0, tiled=True)
    right_side = jnp.einsum("cb,cpk->bpk", owned_blocks, arrived, precision=high).reshape(
        PIX_DEV, channels
    )
    map_cube = jnp.zeros_like(right_side)
    residual = right_side
    direction = right_side
    norm_now = squares(residual)
    applied = operate(direction)
    for iteration in range(ITERS):
        step_size = norm_now / global_sum(jnp.sum(direction * applied))
        map_cube = map_cube + step_size * direction
        residual = residual - step_size * applied
        if iteration == ITERS - 1:
            break
        norm_next = squares(residual)
        applied_residual = operate(residual)
        ratio = norm_next / norm_now
        direction = residual + ratio * direction
        applied = applied_residual + ratio * applied
        norm_now = norm_next
    return (map_cube, residual)


def solution(mesh):
    in_specs = (P("tm", "chan"), P("tm", "chan"), P("tm"), P(), P("chan", None))
    out_specs = (P("tm", "chan"), P("tm", "chan"))
    return jax.shard_map(
        per_device, mesh=mesh, in_specs=in_specs, out_specs=out_specs, check_vma=False
    )
```

```python
import functools

import jax
import jax.numpy as jnp
from jax import lax
from jax.experimental import pallas as pl
from jax.experimental.pallas import tpu as pltpu
from jax.sharding import PartitionSpec as P

PIX_DEV = 512
BLK = 128
ITERS = 3


highest = lax.Precision.HIGHEST
high = lax.Precision.HIGH
ridge = 1.0
RUNS = 4


def gathered(parts_ref, block, hits):
    start = pl.multiple_of(block * BLK, BLK)
    total = None
    for k in range(3):
        term = jnp.dot(hits, parts_ref[k, pl.ds(start, BLK), :], preferred_element_type=jnp.float32)
        total = term if total is None else total + term
    return total


def amp_kernel(blocks_ref, parts_ref, hits_ref, weights_ref, modes_t_ref, amp_ref):
    step = pl.program_id(0)
    for j in range(RUNS):
        x = gathered(parts_ref, blocks_ref[step * RUNS + j], hits_ref[j])
        y = weights_ref[j].astype(jnp.float32) * x
        amp_ref[j] = lax.dot_general(
            modes_t_ref[...], y, (((1,), (1,)), ((), ())),
            precision=highest, preferred_element_type=jnp.float32,
        )


def bin_kernel(blocks_ref, parts_ref, hits_ref, rows_ref, weights_ref, amp_ref, stacked_ref, out_ref):
    step = pl.program_id(0)

    @pl.when(step == 0)
    def _():
        out_ref[...] = jnp.zeros_like(out_ref)

    for j in range(RUNS):
        block = blocks_ref[step * RUNS + j]
        x = gathered(parts_ref, block, hits_ref[j])
        w = weights_ref[j].astype(jnp.float32)
        correction = jnp.dot(amp_ref[j], stacked_ref[...], preferred_element_type=jnp.float32)
        rest = w * (w * x - correction)
        hits = (rows_ref[j] == lax.broadcasted_iota(jnp.int32, (BLK, rest.shape[0]), 0)).astype(
            jnp.bfloat16
        )
        high_part = rest.astype(jnp.bfloat16)
        low_part = (rest - high_part.astype(jnp.float32)).astype(jnp.bfloat16)
        total = jnp.dot(hits, high_part, preferred_element_type=jnp.float32) + jnp.dot(
            hits, low_part, preferred_element_type=jnp.float32
        )
        start = pl.multiple_of(block * BLK, BLK)
        out_ref[pl.ds(start, BLK), :] += total


def split3(value):
    parts = []
    rest = value
    for _ in range(3):
        rounded = lax.reduce_precision(rest, exponent_bits=8, mantissa_bits=7)
        parts.append(rounded.astype(jnp.bfloat16))
        rest = rest - rounded
    return parts


def owner_operator(blocks, field, hits, points_row, noise_weights, modes_t):
    groups, run_length, channels = noise_weights.shape
    modes = modes_t.shape[0]
    steps = groups // RUNS
    parts = jnp.stack(split3(field))
    full = pl.BlockSpec(parts.shape, lambda i, b: (0, 0, 0))
    per_run = lambda *shape: pl.BlockSpec((RUNS,) + shape, lambda i, b: (i, 0, 0))
    gather_flops = groups * 3 * 2 * run_length * BLK * channels
    amps = pl.pallas_call(
        amp_kernel,
        grid_spec=pltpu.PrefetchScalarGridSpec(
            num_scalar_prefetch=1,
            grid=(steps,),
            in_specs=[full, per_run(run_length, BLK), per_run(run_length, channels),
                      pl.BlockSpec(modes_t.shape, lambda i, b: (0, 0))],
            out_specs=per_run(modes, run_length),
        ),
        out_shape=jax.ShapeDtypeStruct((groups, modes, run_length), jnp.float32),
        cost_estimate=pl.CostEstimate(
            flops=gather_flops + groups * 12 * run_length * channels * modes,
            bytes_accessed=noise_weights.size * 2 + field.size * 4,
            transcendentals=0,
        ),
    )(blocks, parts, hits, noise_weights, modes_t)
    amps = chan_sum(amps)
    high, middle, low = split3(jnp.swapaxes(amps, 1, 2))
    amps = jnp.concatenate([high, middle, low, high, middle, high], axis=-1)
    m_high, m_middle, m_low = split3(modes_t)
    stacked = jnp.concatenate([m_high, m_high, m_high, m_middle, m_middle, m_low], axis=0)
    return pl.pallas_call(
        bin_kernel,
        grid_spec=pltpu.PrefetchScalarGridSpec(
            num_scalar_prefetch=1,
            grid=(steps,),
            in_specs=[full, per_run(run_length, BLK), per_run(1, run_length),
                      per_run(run_length, channels), per_run(run_length, 6 * modes),
                      pl.BlockSpec(stacked.shape, lambda i, b: (0, 0))],
            out_specs=pl.BlockSpec(field.shape, lambda i, b: (0, 0)),
        ),
        out_shape=jax.ShapeDtypeStruct(field.shape, jnp.float32),
        cost_estimate=pl.CostEstimate(
            flops=2 * gather_flops + groups * 12 * run_length * channels * modes,
            bytes_accessed=noise_weights.size * 2 + field.size * 8,
            transcendentals=0,
        ),
    )(blocks, parts, hits, points_row, noise_weights, amps, stacked)


def chan_sum(value):
    count = lax.axis_size("chan")
    total = value
    for shift in range(1, count):
        pairs = [(i, (i + shift) % count) for i in range(count)]
        total = total + lax.ppermute(value, "chan", pairs)
    return total


def global_sum(value):
    everyone = lax.axis_size("tm") * lax.axis_size("chan")
    got = lax.all_to_all(
        jnp.broadcast_to(value, (everyone, 1)), ("tm", "chan"), 0, 0, tiled=True
    )
    return jnp.sum(got)


def per_device(streams, weights, pointing, touched, foreground_modes):
    group_count = lax.axis_size("tm")
    owner_index = lax.axis_index("tm")
    sample_count, channels = streams.shape
    run_length = sample_count // group_count
    blocks_each = PIX_DEV // BLK

    scales = weights.reshape(group_count, run_length, channels)
    points = pointing.reshape(group_count, run_length)
    if run_length == channels:
        packed = jnp.concatenate([scales, points.astype(jnp.bfloat16)[:, None, :]], axis=1)
        packed = lax.all_to_all(packed, "tm", 0, 0, tiled=True)
        weights_in = packed[:, :run_length]
        points_in = packed[:, run_length].astype(jnp.int32)
    else:
        weights_in = lax.all_to_all(scales, "tm", 0, 0, tiled=True)
        points_in = lax.all_to_all(points, "tm", 0, 0, tiled=True)

    column = lax.dynamic_index_in_dim(touched, owner_index, axis=1, keepdims=False)
    owned_blocks = (column[:, None] == jnp.arange(blocks_each, dtype=jnp.int32)[None, :]).astype(
        jnp.float32
    )
    pixel_hits = (points_in[:, :, None] == jnp.arange(BLK, dtype=jnp.int32)[None, None, :]).astype(
        jnp.float32
    )
    noise_weights = weights_in.astype(jnp.float32)

    def filtered(samples, noise_weights):
        weighted = noise_weights * samples
        amplitudes = jnp.einsum("csk,km->mcs", weighted, foreground_modes, precision=highest)
        amplitudes = chan_sum(amplitudes)
        return noise_weights * (
            weighted - jnp.einsum("mcs,km->csk", amplitudes, foreground_modes, precision=highest)
        )

    def binned(samples):
        partial_value = jnp.einsum("csp,csk->cpk", pixel_hits, samples, precision=high)
        summed = jnp.einsum("cb,cpk->bpk", owned_blocks, partial_value, precision=high)
        return summed.reshape(PIX_DEV, channels)

    def pointed(field):
        picked = jnp.einsum(
            "cb,bpk->cpk",
            owned_blocks,
            field.reshape(blocks_each, BLK, channels),
            precision=high,
        )
        return jnp.einsum("csp,cpk->csk", pixel_hits, picked, precision=high)

    def squares(vector):
        return global_sum(jnp.sum(vector * vector))

    point_hits = (points_in[:, :, None] == jnp.arange(BLK, dtype=jnp.int32)[None, None, :]).astype(
        jnp.bfloat16
    )
    points_row = points_in[:, None, :]
    modes_t = foreground_modes.T

    def operate(field):
        return (
            owner_operator(column, field, point_hits, points_row, weights_in, modes_t)
            + ridge * field
        )

    local_hits = (points[:, :, None] == jnp.arange(BLK, dtype=jnp.int32)[None, None, :]).astype(
        jnp.float32
    )
    local_noise = filtered(
        streams.astype(jnp.float32).reshape(group_count, run_length, channels),
        scales.astype(jnp.float32),
    )
    local_partial = jnp.einsum("csp,csk->cpk", local_hits, local_noise, precision=high)
    arrived = lax.all_to_all(local_partial, "tm", 0, 0, tiled=True)
    right_side = jnp.einsum("cb,cpk->bpk", owned_blocks, arrived, precision=high).reshape(
        PIX_DEV, channels
    )
    map_cube = jnp.zeros_like(right_side)
    residual = right_side
    direction = right_side
    norm_now = squares(residual)
    applied = operate(direction)
    for iteration in range(ITERS):
        step_size = norm_now / global_sum(jnp.sum(direction * applied))
        map_cube = map_cube + step_size * direction
        residual = residual - step_size * applied
        if iteration == ITERS - 1:
            break
        norm_next = squares(residual)
        applied_residual = operate(residual)
        ratio = norm_next / norm_now
        direction = residual + ratio * direction
        applied = applied_residual + ratio * applied
        norm_now = norm_next
    return (map_cube, residual)


def solution(mesh):
    in_specs = (P("tm", "chan"), P("tm", "chan"), P("tm"), P(), P("chan", None))
    out_specs = (P("tm", "chan"), P("tm", "chan"))
    return jax.shard_map(
        per_device, mesh=mesh, in_specs=in_specs, out_specs=out_specs, check_vma=False
    )
```

```python
import functools

import jax
import jax.numpy as jnp
from jax import lax
from jax.experimental import pallas as pl
from jax.experimental.pallas import tpu as pltpu
from jax.sharding import PartitionSpec as P

PIX_DEV = 512
BLK = 128
ITERS = 3


highest = lax.Precision.HIGHEST
high = lax.Precision.HIGH
ridge = 1.0
RUNS = 4


def gathered(parts_ref, block, hits):
    start = pl.multiple_of(block * BLK, BLK)
    total = None
    for k in range(3):
        term = jnp.dot(hits, parts_ref[k, pl.ds(start, BLK), :], preferred_element_type=jnp.float32)
        total = term if total is None else total + term
    return total


def amp_kernel(blocks_ref, parts_ref, hits_ref, weights_ref, modes_t_ref, amp_ref):
    step = pl.program_id(0)
    for j in range(RUNS):
        x = gathered(parts_ref, blocks_ref[step * RUNS + j], hits_ref[j])
        y = weights_ref[j].astype(jnp.float32) * x
        amp_ref[j] = lax.dot_general(
            modes_t_ref[...], y, (((1,), (1,)), ((), ())),
            precision=highest, preferred_element_type=jnp.float32,
        )


def bin_kernel(blocks_ref, parts_ref, hits_ref, rows_ref, weights_ref, amp_ref, stacked_ref, out_ref):
    step = pl.program_id(0)

    @pl.when(step == 0)
    def _():
        out_ref[...] = jnp.zeros_like(out_ref)

    for j in range(RUNS):
        block = blocks_ref[step * RUNS + j]
        x = gathered(parts_ref, block, hits_ref[j])
        w = weights_ref[j].astype(jnp.float32)
        rest = amp_ref[j]
        pieces = []
        for _ in range(3):
            piece = rest.astype(jnp.bfloat16)
            rest = rest - piece.astype(jnp.float32)
            pieces.append(piece)
        high, middle, low = pieces
        amp_stack = jnp.concatenate([high, middle, low, high, middle, high], axis=0)
        correction = lax.dot_general(
            amp_stack, stacked_ref[...], (((0,), (0,)), ((), ())),
            preferred_element_type=jnp.float32,
        )
        rest = w * (w * x - correction)
        hits = (rows_ref[j] == lax.broadcasted_iota(jnp.int32, (BLK, rest.shape[0]), 0)).astype(
            jnp.bfloat16
        )
        high_part = rest.astype(jnp.bfloat16)
        low_part = (rest - high_part.astype(jnp.float32)).astype(jnp.bfloat16)
        total = jnp.dot(hits, high_part, preferred_element_type=jnp.float32) + jnp.dot(
            hits, low_part, preferred_element_type=jnp.float32
        )
        start = pl.multiple_of(block * BLK, BLK)
        out_ref[pl.ds(start, BLK), :] += total


def split3(value):
    parts = []
    rest = value
    for _ in range(3):
        rounded = lax.reduce_precision(rest, exponent_bits=8, mantissa_bits=7)
        parts.append(rounded.astype(jnp.bfloat16))
        rest = rest - rounded
    return parts


def owner_operator(blocks, field, hits, points_row, noise_weights, modes_t):
    groups, run_length, channels = noise_weights.shape
    modes = modes_t.shape[0]
    steps = groups // RUNS
    parts = jnp.stack(split3(field))
    full = pl.BlockSpec(parts.shape, lambda i, b: (0, 0, 0))
    per_run = lambda *shape: pl.BlockSpec((RUNS,) + shape, lambda i, b: (i, 0, 0))
    gather_flops = groups * 3 * 2 * run_length * BLK * channels
    amps = pl.pallas_call(
        amp_kernel,
        grid_spec=pltpu.PrefetchScalarGridSpec(
            num_scalar_prefetch=1,
            grid=(steps,),
            in_specs=[full, per_run(run_length, BLK), per_run(run_length, channels),
                      pl.BlockSpec(modes_t.shape, lambda i, b: (0, 0))],
            out_specs=per_run(modes, run_length),
        ),
        out_shape=jax.ShapeDtypeStruct((groups, modes, run_length), jnp.float32),
        cost_estimate=pl.CostEstimate(
            flops=gather_flops + groups * 12 * run_length * channels * modes,
            bytes_accessed=noise_weights.size * 2 + field.size * 4,
            transcendentals=0,
        ),
    )(blocks, parts, hits, noise_weights, modes_t)
    amps = chan_sum(amps)
    m_high, m_middle, m_low = split3(modes_t)
    stacked = jnp.concatenate([m_high, m_high, m_high, m_middle, m_middle, m_low], axis=0)
    return pl.pallas_call(
        bin_kernel,
        grid_spec=pltpu.PrefetchScalarGridSpec(
            num_scalar_prefetch=1,
            grid=(steps,),
            in_specs=[full, per_run(run_length, BLK), per_run(1, run_length),
                      per_run(run_length, channels), per_run(modes, run_length),
                      pl.BlockSpec(stacked.shape, lambda i, b: (0, 0))],
            out_specs=pl.BlockSpec(field.shape, lambda i, b: (0, 0)),
        ),
        out_shape=jax.ShapeDtypeStruct(field.shape, jnp.float32),
        cost_estimate=pl.CostEstimate(
            flops=2 * gather_flops + groups * 12 * run_length * channels * modes,
            bytes_accessed=noise_weights.size * 2 + field.size * 8,
            transcendentals=0,
        ),
    )(blocks, parts, hits, points_row, noise_weights, amps, stacked)


def chan_sum(value):
    count = lax.axis_size("chan")
    total = value
    for shift in range(1, count):
        pairs = [(i, (i + shift) % count) for i in range(count)]
        total = total + lax.ppermute(value, "chan", pairs)
    return total


def global_sum(value):
    everyone = lax.axis_size("tm") * lax.axis_size("chan")
    got = lax.all_to_all(
        jnp.broadcast_to(value, (everyone, 1)), ("tm", "chan"), 0, 0, tiled=True
    )
    return jnp.sum(got)


def per_device(streams, weights, pointing, touched, foreground_modes):
    group_count = lax.axis_size("tm")
    owner_index = lax.axis_index("tm")
    sample_count, channels = streams.shape
    run_length = sample_count // group_count
    blocks_each = PIX_DEV // BLK

    scales = weights.reshape(group_count, run_length, channels)
    points = pointing.reshape(group_count, run_length)
    if run_length == channels:
        packed = jnp.concatenate([scales, points.astype(jnp.bfloat16)[:, None, :]], axis=1)
        packed = lax.all_to_all(packed, "tm", 0, 0, tiled=True)
        weights_in = packed[:, :run_length]
        points_in = packed[:, run_length].astype(jnp.int32)
    else:
        weights_in = lax.all_to_all(scales, "tm", 0, 0, tiled=True)
        points_in = lax.all_to_all(points, "tm", 0, 0, tiled=True)

    column = lax.dynamic_index_in_dim(touched, owner_index, axis=1, keepdims=False)
    owned_blocks = (column[:, None] == jnp.arange(blocks_each, dtype=jnp.int32)[None, :]).astype(
        jnp.float32
    )
    pixel_hits = (points_in[:, :, None] == jnp.arange(BLK, dtype=jnp.int32)[None, None, :]).astype(
        jnp.float32
    )
    noise_weights = weights_in.astype(jnp.float32)

    def filtered(samples, noise_weights):
        weighted = noise_weights * samples
        amplitudes = jnp.einsum("csk,km->mcs", weighted, foreground_modes, precision=highest)
        amplitudes = chan_sum(amplitudes)
        return noise_weights * (
            weighted - jnp.einsum("mcs,km->csk", amplitudes, foreground_modes, precision=highest)
        )

    def binned(samples):
        partial_value = jnp.einsum("csp,csk->cpk", pixel_hits, samples, precision=high)
        summed = jnp.einsum("cb,cpk->bpk", owned_blocks, partial_value, precision=high)
        return summed.reshape(PIX_DEV, channels)

    def pointed(field):
        picked = jnp.einsum(
            "cb,bpk->cpk",
            owned_blocks,
            field.reshape(blocks_each, BLK, channels),
            precision=high,
        )
        return jnp.einsum("csp,cpk->csk", pixel_hits, picked, precision=high)

    def squares(vector):
        return global_sum(jnp.sum(vector * vector))

    point_hits = (points_in[:, :, None] == jnp.arange(BLK, dtype=jnp.int32)[None, None, :]).astype(
        jnp.bfloat16
    )
    points_row = points_in[:, None, :]
    modes_t = foreground_modes.T

    def operate(field):
        return (
            owner_operator(column, field, point_hits, points_row, weights_in, modes_t)
            + ridge * field
        )

    local_hits = (points[:, :, None] == jnp.arange(BLK, dtype=jnp.int32)[None, None, :]).astype(
        jnp.float32
    )
    local_noise = filtered(
        streams.astype(jnp.float32).reshape(group_count, run_length, channels),
        scales.astype(jnp.float32),
    )
    local_partial = jnp.einsum("csp,csk->cpk", local_hits, local_noise, precision=high)
    arrived = lax.all_to_all(local_partial, "tm", 0, 0, tiled=True)
    right_side = jnp.einsum("cb,cpk->bpk", owned_blocks, arrived, precision=high).reshape(
        PIX_DEV, channels
    )
    map_cube = jnp.zeros_like(right_side)
    residual = right_side
    direction = right_side
    norm_now = squares(residual)
    applied = operate(direction)
    for iteration in range(ITERS):
        step_size = norm_now / global_sum(jnp.sum(direction * applied))
        map_cube = map_cube + step_size * direction
        residual = residual - step_size * applied
        if iteration == ITERS - 1:
            break
        norm_next = squares(residual)
        applied_residual = operate(residual)
        ratio = norm_next / norm_now
        direction = residual + ratio * direction
        applied = applied_residual + ratio * applied
        norm_now = norm_next
    return (map_cube, residual)


def solution(mesh):
    in_specs = (P("tm", "chan"), P("tm", "chan"), P("tm"), P(), P("chan", None))
    out_specs = (P("tm", "chan"), P("tm", "chan"))
    return jax.shard_map(
        per_device, mesh=mesh, in_specs=in_specs, out_specs=out_specs, check_vma=False
    )
```

```python
import functools

import jax
import jax.numpy as jnp
from jax import lax
from jax.experimental import pallas as pl
from jax.experimental.pallas import tpu as pltpu
from jax.sharding import PartitionSpec as P

PIX_DEV = 512
BLK = 128
ITERS = 3


highest = lax.Precision.HIGHEST
high = lax.Precision.HIGH
ridge = 1.0
RUNS = 4


def gathered(parts_ref, block, hits):
    start = pl.multiple_of(block * BLK, BLK)
    total = None
    for k in range(parts_ref.shape[0]):
        term = jnp.dot(hits, parts_ref[k, pl.ds(start, BLK), :], preferred_element_type=jnp.float32)
        total = term if total is None else total + term
    return total


def amp_kernel(blocks_ref, parts_ref, hits_ref, weights_ref, modes_t_ref, amp_ref):
    step = pl.program_id(0)
    for j in range(RUNS):
        x = gathered(parts_ref, blocks_ref[step * RUNS + j], hits_ref[j])
        y = weights_ref[j].astype(jnp.float32) * x
        amp_ref[j] = lax.dot_general(
            modes_t_ref[...], y, (((1,), (1,)), ((), ())),
            precision=highest, preferred_element_type=jnp.float32,
        )


def bin_kernel(blocks_ref, parts_ref, hits_ref, rows_ref, weights_ref, amp_ref, stacked_ref, out_ref):
    step = pl.program_id(0)

    @pl.when(step == 0)
    def _():
        out_ref[...] = jnp.zeros_like(out_ref)

    for j in range(RUNS):
        block = blocks_ref[step * RUNS + j]
        x = gathered(parts_ref, block, hits_ref[j])
        w = weights_ref[j].astype(jnp.float32)
        rest = amp_ref[j]
        pieces = []
        for _ in range(3):
            piece = rest.astype(jnp.bfloat16)
            rest = rest - piece.astype(jnp.float32)
            pieces.append(piece)
        high, middle, low = pieces
        amp_stack = jnp.concatenate([high, middle, low, high, middle, high], axis=0)
        correction = lax.dot_general(
            amp_stack, stacked_ref[...], (((0,), (0,)), ((), ())),
            preferred_element_type=jnp.float32,
        )
        rest = w * (w * x - correction)
        hits = (rows_ref[j] == lax.broadcasted_iota(jnp.int32, (BLK, rest.shape[0]), 0)).astype(
            jnp.bfloat16
        )
        high_part = rest.astype(jnp.bfloat16)
        low_part = (rest - high_part.astype(jnp.float32)).astype(jnp.bfloat16)
        total = jnp.dot(hits, high_part, preferred_element_type=jnp.float32) + jnp.dot(
            hits, low_part, preferred_element_type=jnp.float32
        )
        start = pl.multiple_of(block * BLK, BLK)
        out_ref[pl.ds(start, BLK), :] += total


def split3(value):
    parts = []
    rest = value
    for _ in range(3):
        rounded = lax.reduce_precision(rest, exponent_bits=8, mantissa_bits=7)
        parts.append(rounded.astype(jnp.bfloat16))
        rest = rest - rounded
    return parts


def owner_operator(blocks, field, hits, points_row, noise_weights, modes_t):
    groups, run_length, channels = noise_weights.shape
    modes = modes_t.shape[0]
    steps = groups // RUNS
    parts = jnp.stack(split3(field)[:2])
    full = pl.BlockSpec(parts.shape, lambda i, b: (0, 0, 0))
    per_run = lambda *shape: pl.BlockSpec((RUNS,) + shape, lambda i, b: (i, 0, 0))
    gather_flops = groups * 2 * 2 * run_length * BLK * channels
    amps = pl.pallas_call(
        amp_kernel,
        grid_spec=pltpu.PrefetchScalarGridSpec(
            num_scalar_prefetch=1,
            grid=(steps,),
            in_specs=[full, per_run(run_length, BLK), per_run(run_length, channels),
                      pl.BlockSpec(modes_t.shape, lambda i, b: (0, 0))],
            out_specs=per_run(modes, run_length),
        ),
        out_shape=jax.ShapeDtypeStruct((groups, modes, run_length), jnp.float32),
        cost_estimate=pl.CostEstimate(
            flops=gather_flops + groups * 12 * run_length * channels * modes,
            bytes_accessed=noise_weights.size * 2 + field.size * 4,
            transcendentals=0,
        ),
    )(blocks, parts, hits, noise_weights, modes_t)
    amps = chan_sum(amps)
    m_high, m_middle, m_low = split3(modes_t)
    stacked = jnp.concatenate([m_high, m_high, m_high, m_middle, m_middle, m_low], axis=0)
    return pl.pallas_call(
        bin_kernel,
        grid_spec=pltpu.PrefetchScalarGridSpec(
            num_scalar_prefetch=1,
            grid=(steps,),
            in_specs=[full, per_run(run_length, BLK), per_run(1, run_length),
                      per_run(run_length, channels), per_run(modes, run_length),
                      pl.BlockSpec(stacked.shape, lambda i, b: (0, 0))],
            out_specs=pl.BlockSpec(field.shape, lambda i, b: (0, 0)),
        ),
        out_shape=jax.ShapeDtypeStruct(field.shape, jnp.float32),
        cost_estimate=pl.CostEstimate(
            flops=2 * gather_flops + groups * 12 * run_length * channels * modes,
            bytes_accessed=noise_weights.size * 2 + field.size * 8,
            transcendentals=0,
        ),
    )(blocks, parts, hits, points_row, noise_weights, amps, stacked)


def chan_sum(value):
    count = lax.axis_size("chan")
    total = value
    for shift in range(1, count):
        pairs = [(i, (i + shift) % count) for i in range(count)]
        total = total + lax.ppermute(value, "chan", pairs)
    return total


def global_sum(value):
    everyone = lax.axis_size("tm") * lax.axis_size("chan")
    got = lax.all_to_all(
        jnp.broadcast_to(value, (everyone, 1)), ("tm", "chan"), 0, 0, tiled=True
    )
    return jnp.sum(got)


def per_device(streams, weights, pointing, touched, foreground_modes):
    group_count = lax.axis_size("tm")
    owner_index = lax.axis_index("tm")
    sample_count, channels = streams.shape
    run_length = sample_count // group_count
    blocks_each = PIX_DEV // BLK

    scales = weights.reshape(group_count, run_length, channels)
    points = pointing.reshape(group_count, run_length)
    if run_length == channels:
        packed = jnp.concatenate([scales, points.astype(jnp.bfloat16)[:, None, :]], axis=1)
        packed = lax.all_to_all(packed, "tm", 0, 0, tiled=True)
        weights_in = packed[:, :run_length]
        points_in = packed[:, run_length].astype(jnp.int32)
    else:
        weights_in = lax.all_to_all(scales, "tm", 0, 0, tiled=True)
        points_in = lax.all_to_all(points, "tm", 0, 0, tiled=True)

    column = lax.dynamic_index_in_dim(touched, owner_index, axis=1, keepdims=False)
    owned_blocks = (column[:, None] == jnp.arange(blocks_each, dtype=jnp.int32)[None, :]).astype(
        jnp.float32
    )
    pixel_hits = (points_in[:, :, None] == jnp.arange(BLK, dtype=jnp.int32)[None, None, :]).astype(
        jnp.float32
    )
    noise_weights = weights_in.astype(jnp.float32)

    def filtered(samples, noise_weights):
        weighted = noise_weights * samples
        amplitudes = jnp.einsum("csk,km->mcs", weighted, foreground_modes, precision=highest)
        amplitudes = chan_sum(amplitudes)
        return noise_weights * (
            weighted - jnp.einsum("mcs,km->csk", amplitudes, foreground_modes, precision=highest)
        )

    def binned(samples):
        partial_value = jnp.einsum("csp,csk->cpk", pixel_hits, samples, precision=high)
        summed = jnp.einsum("cb,cpk->bpk", owned_blocks, partial_value, precision=high)
        return summed.reshape(PIX_DEV, channels)

    def pointed(field):
        picked = jnp.einsum(
            "cb,bpk->cpk",
            owned_blocks,
            field.reshape(blocks_each, BLK, channels),
            precision=high,
        )
        return jnp.einsum("csp,cpk->csk", pixel_hits, picked, precision=high)

    def squares(vector):
        return global_sum(jnp.sum(vector * vector))

    point_hits = (points_in[:, :, None] == jnp.arange(BLK, dtype=jnp.int32)[None, None, :]).astype(
        jnp.bfloat16
    )
    points_row = points_in[:, None, :]
    modes_t = foreground_modes.T

    def operate(field):
        return (
            owner_operator(column, field, point_hits, points_row, weights_in, modes_t)
            + ridge * field
        )

    local_hits = (points[:, :, None] == jnp.arange(BLK, dtype=jnp.int32)[None, None, :]).astype(
        jnp.float32
    )
    local_noise = filtered(
        streams.astype(jnp.float32).reshape(group_count, run_length, channels),
        scales.astype(jnp.float32),
    )
    local_partial = jnp.einsum("csp,csk->cpk", local_hits, local_noise, precision=high)
    arrived = lax.all_to_all(local_partial, "tm", 0, 0, tiled=True)
    right_side = jnp.einsum("cb,cpk->bpk", owned_blocks, arrived, precision=high).reshape(
        PIX_DEV, channels
    )
    map_cube = jnp.zeros_like(right_side)
    residual = right_side
    direction = right_side
    norm_now = squares(residual)
    applied = operate(direction)
    for iteration in range(ITERS):
        step_size = norm_now / global_sum(jnp.sum(direction * applied))
        map_cube = map_cube + step_size * direction
        residual = residual - step_size * applied
        if iteration == ITERS - 1:
            break
        norm_next = squares(residual)
        applied_residual = operate(residual)
        ratio = norm_next / norm_now
        direction = residual + ratio * direction
        applied = applied_residual + ratio * applied
        norm_now = norm_next
    return (map_cube, residual)


def solution(mesh):
    in_specs = (P("tm", "chan"), P("tm", "chan"), P("tm"), P(), P("chan", None))
    out_specs = (P("tm", "chan"), P("tm", "chan"))
    return jax.shard_map(
        per_device, mesh=mesh, in_specs=in_specs, out_specs=out_specs, check_vma=False
    )
```

```python
import functools

import jax
import jax.numpy as jnp
from jax import lax
from jax.experimental import pallas as pl
from jax.experimental.pallas import tpu as pltpu
from jax.sharding import PartitionSpec as P

PIX_DEV = 512
BLK = 128
ITERS = 3


highest = lax.Precision.HIGHEST
high = lax.Precision.HIGH
ridge = 1.0
RUNS = 4


def gathered(parts_ref, block, hits):
    start = pl.multiple_of(block * BLK, BLK)
    total = None
    for k in range(parts_ref.shape[0]):
        term = jnp.dot(hits, parts_ref[k, pl.ds(start, BLK), :], preferred_element_type=jnp.float32)
        total = term if total is None else total + term
    return total


def amp_kernel(offset, blocks_ref, parts_ref, hits_ref, weights_ref, modes_t_ref, amp_ref):
    step = pl.program_id(0) + offset
    for j in range(RUNS):
        x = gathered(parts_ref, blocks_ref[step * RUNS + j], hits_ref[j])
        y = weights_ref[j].astype(jnp.float32) * x
        amp_ref[j] = lax.dot_general(
            modes_t_ref[...], y, (((1,), (1,)), ((), ())),
            precision=highest, preferred_element_type=jnp.float32,
        )


def bin_kernel(offset, blocks_ref, parts_ref, hits_ref, rows_ref, weights_ref, amp_ref, stacked_ref, out_ref):
    step = pl.program_id(0) + offset

    @pl.when(step == offset)
    def _():
        out_ref[...] = jnp.zeros_like(out_ref)

    for j in range(RUNS):
        block = blocks_ref[step * RUNS + j]
        x = gathered(parts_ref, block, hits_ref[j])
        w = weights_ref[j].astype(jnp.float32)
        rest = amp_ref[j]
        pieces = []
        for _ in range(3):
            piece = rest.astype(jnp.bfloat16)
            rest = rest - piece.astype(jnp.float32)
            pieces.append(piece)
        high, middle, low = pieces
        amp_stack = jnp.concatenate([high, middle, low, high, middle, high], axis=0)
        correction = lax.dot_general(
            amp_stack, stacked_ref[...], (((0,), (0,)), ((), ())),
            preferred_element_type=jnp.float32,
        )
        rest = w * (w * x - correction)
        hits = (rows_ref[j] == lax.broadcasted_iota(jnp.int32, (BLK, rest.shape[0]), 0)).astype(
            jnp.bfloat16
        )
        high_part = rest.astype(jnp.bfloat16)
        low_part = (rest - high_part.astype(jnp.float32)).astype(jnp.bfloat16)
        total = jnp.dot(hits, high_part, preferred_element_type=jnp.float32) + jnp.dot(
            hits, low_part, preferred_element_type=jnp.float32
        )
        start = pl.multiple_of(block * BLK, BLK)
        out_ref[pl.ds(start, BLK), :] += total


def split3(value):
    parts = []
    rest = value
    for _ in range(3):
        rounded = lax.reduce_precision(rest, exponent_bits=8, mantissa_bits=7)
        parts.append(rounded.astype(jnp.bfloat16))
        rest = rest - rounded
    return parts


def owner_operator(blocks, field, hits, points_row, noise_weights, modes_t):
    groups, run_length, channels = noise_weights.shape
    modes = modes_t.shape[0]
    steps = groups // RUNS
    parts = jnp.stack(split3(field)[:2])
    full = pl.BlockSpec(parts.shape, lambda i, b: (0, 0, 0))
    gather_flops = groups * 2 * 2 * run_length * BLK * channels
    m_high, m_middle, m_low = split3(modes_t)
    stacked = jnp.concatenate([m_high, m_high, m_high, m_middle, m_middle, m_low], axis=0)
    halves = 2 if steps % 2 == 0 else 1
    span = steps // halves
    binned = None
    for half in range(halves):
        offset = half * span
        per_run = lambda *shape: pl.BlockSpec((RUNS,) + shape, lambda i, b: (i + offset, 0, 0))
        own_run = lambda *shape: pl.BlockSpec((RUNS,) + shape, lambda i, b: (i, 0, 0))
        amps = pl.pallas_call(
            functools.partial(amp_kernel, offset),
            grid_spec=pltpu.PrefetchScalarGridSpec(
                num_scalar_prefetch=1,
                grid=(span,),
                in_specs=[full, per_run(run_length, BLK), per_run(run_length, channels),
                          pl.BlockSpec(modes_t.shape, lambda i, b: (0, 0))],
                out_specs=own_run(modes, run_length),
            ),
            out_shape=jax.ShapeDtypeStruct((span * RUNS, modes, run_length), jnp.float32),
            cost_estimate=pl.CostEstimate(
                flops=(gather_flops + groups * 12 * run_length * channels * modes) // halves,
                bytes_accessed=noise_weights.size * 2 // halves + field.size * 4,
                transcendentals=0,
            ),
        )(blocks, parts, hits, noise_weights, modes_t)
        amps = chan_sum(amps)
        part = pl.pallas_call(
            functools.partial(bin_kernel, offset),
            grid_spec=pltpu.PrefetchScalarGridSpec(
                num_scalar_prefetch=1,
                grid=(span,),
                in_specs=[full, per_run(run_length, BLK), per_run(1, run_length),
                          per_run(run_length, channels), own_run(modes, run_length),
                          pl.BlockSpec(stacked.shape, lambda i, b: (0, 0))],
                out_specs=pl.BlockSpec(field.shape, lambda i, b: (0, 0)),
            ),
            out_shape=jax.ShapeDtypeStruct(field.shape, jnp.float32),
            cost_estimate=pl.CostEstimate(
                flops=(2 * gather_flops + groups * 12 * run_length * channels * modes) // halves,
                bytes_accessed=noise_weights.size * 2 // halves + field.size * 8,
                transcendentals=0,
            ),
        )(blocks, parts, hits, points_row, noise_weights, amps, stacked)
        binned = part if binned is None else binned + part
    return binned


def chan_sum(value):
    count = lax.axis_size("chan")
    total = value
    for shift in range(1, count):
        pairs = [(i, (i + shift) % count) for i in range(count)]
        total = total + lax.ppermute(value, "chan", pairs)
    return total


def global_sum(value):
    everyone = lax.axis_size("tm") * lax.axis_size("chan")
    got = lax.all_to_all(
        jnp.broadcast_to(value, (everyone, 1)), ("tm", "chan"), 0, 0, tiled=True
    )
    return jnp.sum(got)


def per_device(streams, weights, pointing, touched, foreground_modes):
    group_count = lax.axis_size("tm")
    owner_index = lax.axis_index("tm")
    sample_count, channels = streams.shape
    run_length = sample_count // group_count
    blocks_each = PIX_DEV // BLK

    scales = weights.reshape(group_count, run_length, channels)
    points = pointing.reshape(group_count, run_length)
    if run_length == channels:
        packed = jnp.concatenate([scales, points.astype(jnp.bfloat16)[:, None, :]], axis=1)
        packed = lax.all_to_all(packed, "tm", 0, 0, tiled=True)
        weights_in = packed[:, :run_length]
        points_in = packed[:, run_length].astype(jnp.int32)
    else:
        weights_in = lax.all_to_all(scales, "tm", 0, 0, tiled=True)
        points_in = lax.all_to_all(points, "tm", 0, 0, tiled=True)

    column = lax.dynamic_index_in_dim(touched, owner_index, axis=1, keepdims=False)
    owned_blocks = (column[:, None] == jnp.arange(blocks_each, dtype=jnp.int32)[None, :]).astype(
        jnp.float32
    )
    pixel_hits = (points_in[:, :, None] == jnp.arange(BLK, dtype=jnp.int32)[None, None, :]).astype(
        jnp.float32
    )
    noise_weights = weights_in.astype(jnp.float32)

    def filtered(samples, noise_weights):
        weighted = noise_weights * samples
        amplitudes = jnp.einsum("csk,km->mcs", weighted, foreground_modes, precision=highest)
        amplitudes = chan_sum(amplitudes)
        return noise_weights * (
            weighted - jnp.einsum("mcs,km->csk", amplitudes, foreground_modes, precision=highest)
        )

    def binned(samples):
        partial_value = jnp.einsum("csp,csk->cpk", pixel_hits, samples, precision=high)
        summed = jnp.einsum("cb,cpk->bpk", owned_blocks, partial_value, precision=high)
        return summed.reshape(PIX_DEV, channels)

    def pointed(field):
        picked = jnp.einsum(
            "cb,bpk->cpk",
            owned_blocks,
            field.reshape(blocks_each, BLK, channels),
            precision=high,
        )
        return jnp.einsum("csp,cpk->csk", pixel_hits, picked, precision=high)

    def squares(vector):
        return global_sum(jnp.sum(vector * vector))

    point_hits = (points_in[:, :, None] == jnp.arange(BLK, dtype=jnp.int32)[None, None, :]).astype(
        jnp.bfloat16
    )
    points_row = points_in[:, None, :]
    modes_t = foreground_modes.T

    def operate(field):
        return (
            owner_operator(column, field, point_hits, points_row, weights_in, modes_t)
            + ridge * field
        )

    local_hits = (points[:, :, None] == jnp.arange(BLK, dtype=jnp.int32)[None, None, :]).astype(
        jnp.float32
    )
    local_noise = filtered(
        streams.astype(jnp.float32).reshape(group_count, run_length, channels),
        scales.astype(jnp.float32),
    )
    local_partial = jnp.einsum("csp,csk->cpk", local_hits, local_noise, precision=high)
    arrived = lax.all_to_all(local_partial, "tm", 0, 0, tiled=True)
    right_side = jnp.einsum("cb,cpk->bpk", owned_blocks, arrived, precision=high).reshape(
        PIX_DEV, channels
    )
    map_cube = jnp.zeros_like(right_side)
    residual = right_side
    direction = right_side
    norm_now = squares(residual)
    applied = operate(direction)
    for iteration in range(ITERS):
        step_size = norm_now / global_sum(jnp.sum(direction * applied))
        map_cube = map_cube + step_size * direction
        residual = residual - step_size * applied
        if iteration == ITERS - 1:
            break
        norm_next = squares(residual)
        applied_residual = operate(residual)
        ratio = norm_next / norm_now
        direction = residual + ratio * direction
        applied = applied_residual + ratio * applied
        norm_now = norm_next
    return (map_cube, residual)


def solution(mesh):
    in_specs = (P("tm", "chan"), P("tm", "chan"), P("tm"), P(), P("chan", None))
    out_specs = (P("tm", "chan"), P("tm", "chan"))
    return jax.shard_map(
        per_device, mesh=mesh, in_specs=in_specs, out_specs=out_specs, check_vma=False
    )
```

```python
import functools

import jax
import jax.numpy as jnp
from jax import lax
from jax.experimental import pallas as pl
from jax.experimental.pallas import tpu as pltpu
from jax.sharding import PartitionSpec as P

PIX_DEV = 512
BLK = 128
ITERS = 3


highest = lax.Precision.HIGHEST
high = lax.Precision.HIGH
ridge = 1.0
RUNS = 8


def gathered(parts_ref, block, hits):
    start = pl.multiple_of(block * BLK, BLK)
    total = None
    for k in range(parts_ref.shape[0]):
        term = jnp.dot(hits, parts_ref[k, pl.ds(start, BLK), :], preferred_element_type=jnp.float32)
        total = term if total is None else total + term
    return total


def amp_kernel(offset, blocks_ref, parts_ref, hits_ref, weights_ref, modes_t_ref, amp_ref):
    step = pl.program_id(0) + offset
    for j in range(RUNS):
        x = gathered(parts_ref, blocks_ref[step * RUNS + j], hits_ref[j])
        y = weights_ref[j].astype(jnp.float32) * x
        amp_ref[j] = lax.dot_general(
            modes_t_ref[...], y, (((1,), (1,)), ((), ())),
            precision=highest, preferred_element_type=jnp.float32,
        )


def bin_kernel(offset, blocks_ref, parts_ref, hits_ref, rows_ref, weights_ref, amp_ref, stacked_ref, out_ref):
    step = pl.program_id(0) + offset

    @pl.when(step == offset)
    def _():
        out_ref[...] = jnp.zeros_like(out_ref)

    for j in range(RUNS):
        block = blocks_ref[step * RUNS + j]
        x = gathered(parts_ref, block, hits_ref[j])
        w = weights_ref[j].astype(jnp.float32)
        rest = amp_ref[j]
        pieces = []
        for _ in range(3):
            piece = rest.astype(jnp.bfloat16)
            rest = rest - piece.astype(jnp.float32)
            pieces.append(piece)
        high, middle, low = pieces
        amp_stack = jnp.concatenate([high, middle, low, high, middle, high], axis=0)
        correction = lax.dot_general(
            amp_stack, stacked_ref[...], (((0,), (0,)), ((), ())),
            preferred_element_type=jnp.float32,
        )
        rest = w * (w * x - correction)
        hits = (rows_ref[j] == lax.broadcasted_iota(jnp.int32, (BLK, rest.shape[0]), 0)).astype(
            jnp.bfloat16
        )
        high_part = rest.astype(jnp.bfloat16)
        low_part = (rest - high_part.astype(jnp.float32)).astype(jnp.bfloat16)
        total = jnp.dot(hits, high_part, preferred_element_type=jnp.float32) + jnp.dot(
            hits, low_part, preferred_element_type=jnp.float32
        )
        start = pl.multiple_of(block * BLK, BLK)
        out_ref[pl.ds(start, BLK), :] += total


def split3(value):
    parts = []
    rest = value
    for _ in range(3):
        rounded = lax.reduce_precision(rest, exponent_bits=8, mantissa_bits=7)
        parts.append(rounded.astype(jnp.bfloat16))
        rest = rest - rounded
    return parts


def owner_operator(blocks, field, hits, points_row, noise_weights, modes_t):
    groups, run_length, channels = noise_weights.shape
    modes = modes_t.shape[0]
    steps = groups // RUNS
    parts = jnp.stack(split3(field)[:2])
    full = pl.BlockSpec(parts.shape, lambda i, b: (0, 0, 0))
    gather_flops = groups * 2 * 2 * run_length * BLK * channels
    m_high, m_middle, m_low = split3(modes_t)
    stacked = jnp.concatenate([m_high, m_high, m_high, m_middle, m_middle, m_low], axis=0)
    halves = 2 if steps % 2 == 0 else 1
    span = steps // halves
    binned = None
    for half in range(halves):
        offset = half * span
        per_run = lambda *shape: pl.BlockSpec((RUNS,) + shape, lambda i, b: (i + offset, 0, 0))
        own_run = lambda *shape: pl.BlockSpec((RUNS,) + shape, lambda i, b: (i, 0, 0))
        amps = pl.pallas_call(
            functools.partial(amp_kernel, offset),
            grid_spec=pltpu.PrefetchScalarGridSpec(
                num_scalar_prefetch=1,
                grid=(span,),
                in_specs=[full, per_run(run_length, BLK), per_run(run_length, channels),
                          pl.BlockSpec(modes_t.shape, lambda i, b: (0, 0))],
                out_specs=own_run(modes, run_length),
            ),
            out_shape=jax.ShapeDtypeStruct((span * RUNS, modes, run_length), jnp.float32),
            cost_estimate=pl.CostEstimate(
                flops=(gather_flops + groups * 12 * run_length * channels * modes) // halves,
                bytes_accessed=noise_weights.size * 2 // halves + field.size * 4,
                transcendentals=0,
            ),
        )(blocks, parts, hits, noise_weights, modes_t)
        amps = chan_sum(amps)
        part = pl.pallas_call(
            functools.partial(bin_kernel, offset),
            grid_spec=pltpu.PrefetchScalarGridSpec(
                num_scalar_prefetch=1,
                grid=(span,),
                in_specs=[full, per_run(run_length, BLK), per_run(1, run_length),
                          per_run(run_length, channels), own_run(modes, run_length),
                          pl.BlockSpec(stacked.shape, lambda i, b: (0, 0))],
                out_specs=pl.BlockSpec(field.shape, lambda i, b: (0, 0)),
            ),
            out_shape=jax.ShapeDtypeStruct(field.shape, jnp.float32),
            cost_estimate=pl.CostEstimate(
                flops=(2 * gather_flops + groups * 12 * run_length * channels * modes) // halves,
                bytes_accessed=noise_weights.size * 2 // halves + field.size * 8,
                transcendentals=0,
            ),
        )(blocks, parts, hits, points_row, noise_weights, amps, stacked)
        binned = part if binned is None else binned + part
    return binned


def chan_sum(value):
    count = lax.axis_size("chan")
    total = value
    for shift in range(1, count):
        pairs = [(i, (i + shift) % count) for i in range(count)]
        total = total + lax.ppermute(value, "chan", pairs)
    return total


def global_sum(value):
    everyone = lax.axis_size("tm") * lax.axis_size("chan")
    got = lax.all_to_all(
        jnp.broadcast_to(value, (everyone, 1)), ("tm", "chan"), 0, 0, tiled=True
    )
    return jnp.sum(got)


def per_device(streams, weights, pointing, touched, foreground_modes):
    group_count = lax.axis_size("tm")
    owner_index = lax.axis_index("tm")
    sample_count, channels = streams.shape
    run_length = sample_count // group_count
    blocks_each = PIX_DEV // BLK

    scales = weights.reshape(group_count, run_length, channels)
    points = pointing.reshape(group_count, run_length)
    if run_length == channels:
        packed = jnp.concatenate([scales, points.astype(jnp.bfloat16)[:, None, :]], axis=1)
        packed = lax.all_to_all(packed, "tm", 0, 0, tiled=True)
        weights_in = packed[:, :run_length]
        points_in = packed[:, run_length].astype(jnp.int32)
    else:
        weights_in = lax.all_to_all(scales, "tm", 0, 0, tiled=True)
        points_in = lax.all_to_all(points, "tm", 0, 0, tiled=True)

    column = lax.dynamic_index_in_dim(touched, owner_index, axis=1, keepdims=False)
    owned_blocks = (column[:, None] == jnp.arange(blocks_each, dtype=jnp.int32)[None, :]).astype(
        jnp.float32
    )
    pixel_hits = (points_in[:, :, None] == jnp.arange(BLK, dtype=jnp.int32)[None, None, :]).astype(
        jnp.float32
    )
    noise_weights = weights_in.astype(jnp.float32)

    def filtered(samples, noise_weights):
        weighted = noise_weights * samples
        amplitudes = jnp.einsum("csk,km->mcs", weighted, foreground_modes, precision=highest)
        amplitudes = chan_sum(amplitudes)
        return noise_weights * (
            weighted - jnp.einsum("mcs,km->csk", amplitudes, foreground_modes, precision=highest)
        )

    def binned(samples):
        partial_value = jnp.einsum("csp,csk->cpk", pixel_hits, samples, precision=high)
        summed = jnp.einsum("cb,cpk->bpk", owned_blocks, partial_value, precision=high)
        return summed.reshape(PIX_DEV, channels)

    def pointed(field):
        picked = jnp.einsum(
            "cb,bpk->cpk",
            owned_blocks,
            field.reshape(blocks_each, BLK, channels),
            precision=high,
        )
        return jnp.einsum("csp,cpk->csk", pixel_hits, picked, precision=high)

    def squares(vector):
        return global_sum(jnp.sum(vector * vector))

    point_hits = (points_in[:, :, None] == jnp.arange(BLK, dtype=jnp.int32)[None, None, :]).astype(
        jnp.bfloat16
    )
    points_row = points_in[:, None, :]
    modes_t = foreground_modes.T

    def operate(field):
        return (
            owner_operator(column, field, point_hits, points_row, weights_in, modes_t)
            + ridge * field
        )

    local_hits = (points[:, :, None] == jnp.arange(BLK, dtype=jnp.int32)[None, None, :]).astype(
        jnp.float32
    )
    local_noise = filtered(
        streams.astype(jnp.float32).reshape(group_count, run_length, channels),
        scales.astype(jnp.float32),
    )
    local_partial = jnp.einsum("csp,csk->cpk", local_hits, local_noise, precision=high)
    arrived = lax.all_to_all(local_partial, "tm", 0, 0, tiled=True)
    right_side = jnp.einsum("cb,cpk->bpk", owned_blocks, arrived, precision=high).reshape(
        PIX_DEV, channels
    )
    map_cube = jnp.zeros_like(right_side)
    residual = right_side
    direction = right_side
    norm_now = squares(residual)
    applied = operate(direction)
    for iteration in range(ITERS):
        step_size = norm_now / global_sum(jnp.sum(direction * applied))
        map_cube = map_cube + step_size * direction
        residual = residual - step_size * applied
        if iteration == ITERS - 1:
            break
        norm_next = squares(residual)
        applied_residual = operate(residual)
        ratio = norm_next / norm_now
        direction = residual + ratio * direction
        applied = applied_residual + ratio * applied
        norm_now = norm_next
    return (map_cube, residual)


def solution(mesh):
    in_specs = (P("tm", "chan"), P("tm", "chan"), P("tm"), P(), P("chan", None))
    out_specs = (P("tm", "chan"), P("tm", "chan"))
    return jax.shard_map(
        per_device, mesh=mesh, in_specs=in_specs, out_specs=out_specs, check_vma=False
    )
```

```python
import functools

import jax
import jax.numpy as jnp
from jax import lax
from jax.experimental import pallas as pl
from jax.experimental.pallas import tpu as pltpu
from jax.sharding import PartitionSpec as P

PIX_DEV = 512
BLK = 128
ITERS = 3


highest = lax.Precision.HIGHEST
high = lax.Precision.HIGH
ridge = 1.0
RUNS = 8


def gathered(parts_ref, block, hits):
    start = pl.multiple_of(block * BLK, BLK)
    total = None
    for k in range(parts_ref.shape[0]):
        term = jnp.dot(hits, parts_ref[k, pl.ds(start, BLK), :], preferred_element_type=jnp.float32)
        total = term if total is None else total + term
    return total


def amp_kernel(offset, blocks_ref, parts_ref, hits_ref, weights_ref, modes_t_ref, amp_ref):
    step = pl.program_id(0) + offset
    for j in range(RUNS):
        x = gathered(parts_ref, blocks_ref[step * RUNS + j], hits_ref[j])
        y = weights_ref[j].astype(jnp.float32) * x
        amp_ref[j] = lax.dot_general(
            modes_t_ref[...], y, (((1,), (1,)), ((), ())),
            precision=highest, preferred_element_type=jnp.float32,
        )


def bin_kernel(offset, blocks_ref, parts_ref, hits_ref, rows_ref, weights_ref, amp_ref, stacked_ref, out_ref):
    step = pl.program_id(0) + offset

    @pl.when(step == offset)
    def _():
        out_ref[...] = jnp.zeros_like(out_ref)

    for j in range(RUNS):
        block = blocks_ref[step * RUNS + j]
        x = gathered(parts_ref, block, hits_ref[j])
        w = weights_ref[j].astype(jnp.float32)
        rest = amp_ref[j]
        pieces = []
        for _ in range(3):
            piece = rest.astype(jnp.bfloat16)
            rest = rest - piece.astype(jnp.float32)
            pieces.append(piece)
        high, middle, low = pieces
        amp_stack = jnp.concatenate([high, middle, low, high, middle, high], axis=0)
        correction = lax.dot_general(
            amp_stack, stacked_ref[...], (((0,), (0,)), ((), ())),
            preferred_element_type=jnp.float32,
        )
        rest = w * (w * x - correction)
        hits = (rows_ref[j] == lax.broadcasted_iota(jnp.int32, (BLK, rest.shape[0]), 0)).astype(
            jnp.bfloat16
        )
        high_part = rest.astype(jnp.bfloat16)
        low_part = (rest - high_part.astype(jnp.float32)).astype(jnp.bfloat16)
        total = jnp.dot(hits, high_part, preferred_element_type=jnp.float32) + jnp.dot(
            hits, low_part, preferred_element_type=jnp.float32
        )
        start = pl.multiple_of(block * BLK, BLK)
        out_ref[pl.ds(start, BLK), :] += total


def split3(value):
    parts = []
    rest = value
    for _ in range(3):
        rounded = lax.reduce_precision(rest, exponent_bits=8, mantissa_bits=7)
        parts.append(rounded.astype(jnp.bfloat16))
        rest = rest - rounded
    return parts


def owner_operator(blocks, field, hits, points_row, noise_weights, modes_t):
    groups, run_length, channels = noise_weights.shape
    modes = modes_t.shape[0]
    steps = groups // RUNS
    parts = jnp.stack(split3(field)[:2])
    full = pl.BlockSpec(parts.shape, lambda i, b: (0, 0, 0))
    gather_flops = groups * 2 * 2 * run_length * BLK * channels
    m_high, m_middle, m_low = split3(modes_t)
    stacked = jnp.concatenate([m_high, m_high, m_high, m_middle, m_middle, m_low], axis=0)
    halves = 4 if steps % 4 == 0 else (2 if steps % 2 == 0 else 1)
    span = steps // halves
    binned = None
    for half in range(halves):
        offset = half * span
        per_run = lambda *shape: pl.BlockSpec((RUNS,) + shape, lambda i, b: (i + offset, 0, 0))
        own_run = lambda *shape: pl.BlockSpec((RUNS,) + shape, lambda i, b: (i, 0, 0))
        amps = pl.pallas_call(
            functools.partial(amp_kernel, offset),
            grid_spec=pltpu.PrefetchScalarGridSpec(
                num_scalar_prefetch=1,
                grid=(span,),
                in_specs=[full, per_run(run_length, BLK), per_run(run_length, channels),
                          pl.BlockSpec(modes_t.shape, lambda i, b: (0, 0))],
                out_specs=own_run(modes, run_length),
            ),
            out_shape=jax.ShapeDtypeStruct((span * RUNS, modes, run_length), jnp.float32),
            cost_estimate=pl.CostEstimate(
                flops=(gather_flops + groups * 12 * run_length * channels * modes) // halves,
                bytes_accessed=noise_weights.size * 2 // halves + field.size * 4,
                transcendentals=0,
            ),
        )(blocks, parts, hits, noise_weights, modes_t)
        amps = chan_sum(amps)
        part = pl.pallas_call(
            functools.partial(bin_kernel, offset),
            grid_spec=pltpu.PrefetchScalarGridSpec(
                num_scalar_prefetch=1,
                grid=(span,),
                in_specs=[full, per_run(run_length, BLK), per_run(1, run_length),
                          per_run(run_length, channels), own_run(modes, run_length),
                          pl.BlockSpec(stacked.shape, lambda i, b: (0, 0))],
                out_specs=pl.BlockSpec(field.shape, lambda i, b: (0, 0)),
            ),
            out_shape=jax.ShapeDtypeStruct(field.shape, jnp.float32),
            cost_estimate=pl.CostEstimate(
                flops=(2 * gather_flops + groups * 12 * run_length * channels * modes) // halves,
                bytes_accessed=noise_weights.size * 2 // halves + field.size * 8,
                transcendentals=0,
            ),
        )(blocks, parts, hits, points_row, noise_weights, amps, stacked)
        binned = part if binned is None else binned + part
    return binned


def chan_sum(value):
    count = lax.axis_size("chan")
    total = value
    for shift in range(1, count):
        pairs = [(i, (i + shift) % count) for i in range(count)]
        total = total + lax.ppermute(value, "chan", pairs)
    return total


def global_sum(value):
    everyone = lax.axis_size("tm") * lax.axis_size("chan")
    got = lax.all_to_all(
        jnp.broadcast_to(value, (everyone, 1)), ("tm", "chan"), 0, 0, tiled=True
    )
    return jnp.sum(got)


def per_device(streams, weights, pointing, touched, foreground_modes):
    group_count = lax.axis_size("tm")
    owner_index = lax.axis_index("tm")
    sample_count, channels = streams.shape
    run_length = sample_count // group_count
    blocks_each = PIX_DEV // BLK

    scales = weights.reshape(group_count, run_length, channels)
    points = pointing.reshape(group_count, run_length)
    if run_length == channels:
        packed = jnp.concatenate([scales, points.astype(jnp.bfloat16)[:, None, :]], axis=1)
        packed = lax.all_to_all(packed, "tm", 0, 0, tiled=True)
        weights_in = packed[:, :run_length]
        points_in = packed[:, run_length].astype(jnp.int32)
    else:
        weights_in = lax.all_to_all(scales, "tm", 0, 0, tiled=True)
        points_in = lax.all_to_all(points, "tm", 0, 0, tiled=True)

    column = lax.dynamic_index_in_dim(touched, owner_index, axis=1, keepdims=False)
    owned_blocks = (column[:, None] == jnp.arange(blocks_each, dtype=jnp.int32)[None, :]).astype(
        jnp.float32
    )
    pixel_hits = (points_in[:, :, None] == jnp.arange(BLK, dtype=jnp.int32)[None, None, :]).astype(
        jnp.float32
    )
    noise_weights = weights_in.astype(jnp.float32)

    def filtered(samples, noise_weights):
        weighted = noise_weights * samples
        amplitudes = jnp.einsum("csk,km->mcs", weighted, foreground_modes, precision=highest)
        amplitudes = chan_sum(amplitudes)
        return noise_weights * (
            weighted - jnp.einsum("mcs,km->csk", amplitudes, foreground_modes, precision=highest)
        )

    def binned(samples):
        partial_value = jnp.einsum("csp,csk->cpk", pixel_hits, samples, precision=high)
        summed = jnp.einsum("cb,cpk->bpk", owned_blocks, partial_value, precision=high)
        return summed.reshape(PIX_DEV, channels)

    def pointed(field):
        picked = jnp.einsum(
            "cb,bpk->cpk",
            owned_blocks,
            field.reshape(blocks_each, BLK, channels),
            precision=high,
        )
        return jnp.einsum("csp,cpk->csk", pixel_hits, picked, precision=high)

    def squares(vector):
        return global_sum(jnp.sum(vector * vector))

    point_hits = (points_in[:, :, None] == jnp.arange(BLK, dtype=jnp.int32)[None, None, :]).astype(
        jnp.bfloat16
    )
    points_row = points_in[:, None, :]
    modes_t = foreground_modes.T

    def operate(field):
        return (
            owner_operator(column, field, point_hits, points_row, weights_in, modes_t)
            + ridge * field
        )

    local_hits = (points[:, :, None] == jnp.arange(BLK, dtype=jnp.int32)[None, None, :]).astype(
        jnp.float32
    )
    local_noise = filtered(
        streams.astype(jnp.float32).reshape(group_count, run_length, channels),
        scales.astype(jnp.float32),
    )
    local_partial = jnp.einsum("csp,csk->cpk", local_hits, local_noise, precision=high)
    arrived = lax.all_to_all(local_partial, "tm", 0, 0, tiled=True)
    right_side = jnp.einsum("cb,cpk->bpk", owned_blocks, arrived, precision=high).reshape(
        PIX_DEV, channels
    )
    map_cube = jnp.zeros_like(right_side)
    residual = right_side
    direction = right_side
    norm_now = squares(residual)
    applied = operate(direction)
    for iteration in range(ITERS):
        step_size = norm_now / global_sum(jnp.sum(direction * applied))
        map_cube = map_cube + step_size * direction
        residual = residual - step_size * applied
        if iteration == ITERS - 1:
            break
        norm_next = squares(residual)
        applied_residual = operate(residual)
        ratio = norm_next / norm_now
        direction = residual + ratio * direction
        applied = applied_residual + ratio * applied
        norm_now = norm_next
    return (map_cube, residual)


def solution(mesh):
    in_specs = (P("tm", "chan"), P("tm", "chan"), P("tm"), P(), P("chan", None))
    out_specs = (P("tm", "chan"), P("tm", "chan"))
    return jax.shard_map(
        per_device, mesh=mesh, in_specs=in_specs, out_specs=out_specs, check_vma=False
    )
```
